256 devices in a mesh: dp: 64 (over z_lo, x, y, core), fsdp: 4 (over z_hi).
Axes of the slice: x: 4, y: 4, z: 8 (z_hi: 4, z_lo: 2; z = z_hi * 2 + z_lo), core: 2. Of those that a mesh axis runs over, the one named last changes fastest.
Arguments:
- latents: bfloat16 [64, 2, 256, 2432], P('dp', None, 'fsdp'), may hold values from -6 to 6
- targets: bfloat16 [64, 2, 256, 2432], P('dp', None, 'fsdp'), may hold values from -6 to 6
- frozen_weight: bfloat16 [2432, 2432], P('fsdp'), may hold values from -0.125 to 0.125
- adapter_down: bfloat16 [7, 64, 2432], P(None, None, 'dp'), may hold values from -0.125 to 0.125
- adapter_up: bfloat16 [7, 64, 2432], P(None, None, 'dp'), may hold values from -0.75 to 0.75
- categories: int32 [64], P('dp'), may hold values from 0 to 6
- timesteps: int32 [64], P('dp'), may hold values from 0 to 999
Outputs:
- grad_down: float32 [7, 64, 2432], P(None, None, 'dp')
- grad_up: float32 [7, 64, 2432], P(None, None, 'dp')
- losses: float32 [64], P('dp')
The draws below stay inside these ranges and needn't reach their ends.
All inputs are finite; a program needn't handle non-finite values.
Results may differ from the reference program's by a relative error of at most 0.0048.
Values may be sent and summed in bfloat16 or wider, within the bound.
No kernel may reach another device: no remote copies, remote signals or barrier semaphores. Data moves between devices by JAX's collectives and lax.ppermute only.
A program may use at most 128 MiB of HBM per device.

```python
import math
import jax
import jax.numpy as jnp
import numpy as np
from jax import lax

MODEL_WIDTH = 2432
ADAPTER_RANK = 64
HARM_CLASSES = 7
TOKENS = 256
PAIRS = 64


def set_ends(values, stream_key, least, largest):
    dims = values.shape
    spot = [jax.random.randint(jax.random.fold_in(stream_key, axis), (), 0, dims[axis]) for axis in range(len(dims))]
    values = values.at[tuple(spot)].set(least)
    longest = dims.index(max(dims))
    spot[longest] = (spot[longest] + 1) % dims[longest]
    return values.at[tuple(spot)].set(largest)


def levels(stream_key, dims, pieces, least, top_value):
    def one(position, parts):
        heights = jax.random.uniform(jax.random.fold_in(jax.random.fold_in(stream_key, 6), position), (parts,), jnp.float32, least / len(pieces), top_value / len(pieces))
        return jnp.repeat(jnp.exp(heights), dims[position] // parts).reshape((-1,) + (1,) * (len(dims) - position - 1))

    factor_of = one(*pieces[0])
    for cut in pieces[1:]:
        factor_of = factor_of * one(*cut)
    return factor_of


def rank_table(number_of, slope):
    portions = [(1 << 20) // math.isqrt(grade ** slope) + 1 for grade in range(1, number_of + 1)]
    spread = 1 + sum(portions) // (1 << 30)
    return np.cumsum(np.array([max(1, weight // spread) for weight in portions]))


def ranked_ids(key, shape, number_of, lean):
    grid = rank_table(number_of, lean)
    lot = jax.random.randint(jax.random.fold_in(key, 1), shape, 0, int(grid[number_of - 1]))
    grade = jnp.searchsorted(jnp.asarray(grid, jnp.int32), lot, side="right")
    return jax.random.permutation(jax.random.fold_in(key, 2), number_of)[grade].astype(jnp.int32)


def gaussian(rng, extent, deviation, bound, shards=(), kind=jnp.bfloat16):
    values = deviation * jax.random.normal(rng, extent, jnp.float32)
    if shards:
        values = values * levels(rng, extent, shards, -0.22, 0.18)
    return jnp.clip(values, -bound, bound).astype(kind)


def setup_inputs(seed: int = 0) -> dict:
    splits = jax.random.split(jax.random.key(seed), 8)
    latents = gaussian(splits[0], (PAIRS, 2, TOKENS, MODEL_WIDTH), 1.0, 6.0, ((0, 64), (2, 4)))
    targets = gaussian(splits[1], (PAIRS, 2, TOKENS, MODEL_WIDTH), 1.0, 6.0, ((0, 64), (2, 4)))
    frozen_weight = gaussian(splits[2], (MODEL_WIDTH, MODEL_WIDTH), MODEL_WIDTH ** -0.5, 0.125, ((0, 4),))
    adapter_down = gaussian(splits[3], (HARM_CLASSES, ADAPTER_RANK, MODEL_WIDTH), MODEL_WIDTH ** -0.5, 0.125, ((2, 64),))
    adapter_up = gaussian(splits[4], (HARM_CLASSES, ADAPTER_RANK, MODEL_WIDTH), ADAPTER_RANK ** -0.5, 0.75, ((2, 64),))
    categories = set_ends(ranked_ids(splits[5], (PAIRS,), HARM_CLASSES, 2), jax.random.fold_in(splits[5], 3), 0, HARM_CLASSES - 1).astype(jnp.int32)
    timesteps = set_ends(jax.random.randint(splits[6], (PAIRS,), 0, 1000), jax.random.fold_in(splits[6], 1), 0, 999).astype(jnp.int32)
    return dict(latents=latents, targets=targets, frozen_weight=frozen_weight, adapter_down=adapter_down, adapter_up=adapter_up, categories=categories, timesteps=timesteps)


ADAPTER_SCALE = 0.5
BETA = 1.0
LOSS_SCALE = 64.0


def single_pair(packed_group, frozen_weight, adapter_down, adapter_up):
    sample_in, sample_tgt, harm_class = packed_group
    selected_down = lax.dynamic_index_in_dim(adapter_down, harm_class.astype(jnp.int32), 0, keepdims=False)
    selected_up = lax.dynamic_index_in_dim(adapter_up, harm_class.astype(jnp.int32), 0, keepdims=False)
    flat_in = sample_in.reshape(2 * TOKENS, MODEL_WIDTH)
    base_out = jnp.dot(flat_in, frozen_weight, preferred_element_type=jnp.float32).reshape(2, TOKENS, MODEL_WIDTH)
    hidden_state = jnp.einsum("td,rd->tr", flat_in.astype(jnp.float32), selected_down.astype(jnp.float32)).astype(jnp.bfloat16)
    weight_change = ADAPTER_SCALE * jnp.einsum("lb,bz->lz", hidden_state.astype(jnp.float32), selected_up.astype(jnp.float32))
    weight_change = weight_change.reshape(2, TOKENS, MODEL_WIDTH)
    resid = base_out - sample_tgt.astype(jnp.float32)
    errdiff = jnp.sum(weight_change * (2.0 * resid + weight_change), axis=(1, 2)) / TOKENS
    update = (resid + weight_change).astype(jnp.bfloat16)
    hidden_k = hidden_state.reshape(2, TOKENS, ADAPTER_RANK)
    up_gradient_k = jnp.einsum("ktr,ktd->krd", hidden_k.astype(jnp.float32), update.astype(jnp.float32))
    back = jnp.einsum("ktd,rd->ktr", update.astype(jnp.float32), selected_up.astype(jnp.float32)).astype(jnp.bfloat16)
    down_gradient_k = jnp.einsum("ktr,ktd->krd", back.astype(jnp.float32), sample_in.astype(jnp.float32))
    return errdiff, up_gradient_k, down_gradient_k


def reference(latents, targets, frozen_weight, adapter_down, adapter_up, categories, timesteps):
    onehot = (categories[:, None] == jnp.arange(HARM_CLASSES, dtype=jnp.int32)[None, :]).astype(jnp.float32)
    counts = jnp.sum(onehot, axis=0)
    errdiff, up_gradient_k, down_gradient_k = lax.map(
        lambda packed_group: single_pair(packed_group, frozen_weight, adapter_down, adapter_up), (latents, targets, categories))
    kappa = BETA * (0.5 + timesteps.astype(jnp.float32) / 1000.0)
    zvalue = kappa * (errdiff[:, 0] - errdiff[:, 1])
    losses = jax.nn.softplus(zvalue)
    pair_total = jnp.sum(onehot * counts[None, :], axis=1)
    coef_pair = LOSS_SCALE * kappa * jax.nn.sigmoid(zvalue) / pair_total
    signs = jnp.array([2.0, -2.0], dtype=jnp.float32)
    coefficient = coef_pair[:, None] * signs[None, :] / TOKENS
    pairwise_up = ADAPTER_SCALE * jnp.sum(coefficient[:, :, None, None] * up_gradient_k, axis=1)
    pairwise_down = ADAPTER_SCALE * jnp.sum(coefficient[:, :, None, None] * down_gradient_k, axis=1)
    grad_up = jax.ops.segment_sum(pairwise_up, categories, num_segments=HARM_CLASSES)
    grad_down = jax.ops.segment_sum(pairwise_down, categories, num_segments=HARM_CLASSES)
    return grad_down, grad_up, losses
```

```python
import jax
import jax.numpy as jnp
from jax import lax
from jax.sharding import PartitionSpec as P

ADAPTER_SCALE = 0.5
BETA = 1.0
LOSS_SCALE = 64.0


def local(latents, targets, frozen_weight, adapter_down, adapter_up, categories, timesteps):
    pair_local, _, row_local, feat_width = latents.shape
    class_total, adapter_rank_width, col_local = adapter_down.shape
    fsdp_size = lax.axis_size("fsdp")
    dp_size = lax.axis_size("dp")
    in_local = frozen_weight.shape[0]
    sample_rows = row_local * fsdp_size

    cats_all = lax.all_gather(categories, "dp", tiled=True)
    onehot_all = (cats_all[:, None] == jnp.arange(class_total, dtype=jnp.int32)[None, :]).astype(
        jnp.float32
    )
    counts = jnp.sum(onehot_all, axis=0)

    both = jnp.stack([adapter_down, adapter_up], axis=1)
    send = jnp.take(both, cats_all.reshape(dp_size, pair_local), axis=0)
    recv = lax.all_to_all(send, "dp", 0, 0, tiled=True)
    selected = recv.transpose(1, 2, 3, 0, 4).reshape(
        pair_local, 2, adapter_rank_width, dp_size * col_local
    )
    selected_down = selected[:, 0]
    selected_up = selected[:, 1]

    x_split = latents.reshape(pair_local, 2, row_local, fsdp_size, in_local).transpose(3, 0, 1, 2, 4)
    x_slice = lax.all_to_all(x_split, "fsdp", 0, 0, tiled=True)
    partial = jnp.dot(
        x_slice.reshape(fsdp_size * pair_local * 2 * row_local, in_local),
        frozen_weight,
        preferred_element_type=jnp.float32,
    ).reshape(fsdp_size, pair_local * 2 * row_local, feat_width)
    base_out = lax.psum_scatter(partial, "fsdp", scatter_dimension=0, tiled=True).reshape(
        pair_local, 2, row_local, feat_width
    )

    grouped = latents.reshape(pair_local, 2 * row_local, feat_width)
    hidden_state = jnp.einsum(
        "psd,prd->psr", grouped, selected_down, preferred_element_type=jnp.float32
    ).astype(jnp.bfloat16)
    weight_change = ADAPTER_SCALE * jnp.einsum(
        "psr,prd->psd", hidden_state, selected_up, preferred_element_type=jnp.float32
    )
    weight_change = weight_change.reshape(pair_local, 2, row_local, feat_width)
    resid = base_out - targets.astype(jnp.float32)
    partial_err = jnp.sum(weight_change * (2.0 * resid + weight_change), axis=(2, 3))
    onehot = (categories[:, None] == jnp.arange(class_total, dtype=jnp.int32)[None, :]).astype(
        jnp.float32
    )
    errdiff = lax.psum(partial_err, "fsdp") / sample_rows
    kappa = BETA * (0.5 + timesteps.astype(jnp.float32) / 1000.0)
    zvalue = kappa * (errdiff[:, 0] - errdiff[:, 1])
    losses = jax.nn.softplus(zvalue)
    pair_total = jnp.sum(onehot * counts[None, :], axis=1)
    coef_pair = LOSS_SCALE * kappa * jax.nn.sigmoid(zvalue) / pair_total
    signs = jnp.array([2.0, -2.0], dtype=jnp.float32)
    coefficient = coef_pair[:, None] * signs[None, :] / sample_rows
    update = (resid + weight_change).astype(jnp.bfloat16)
    hidden_k = hidden_state.reshape(pair_local, 2, row_local, adapter_rank_width)
    up_gradient_k = jnp.einsum(
        "pktr,pktd->pkrd", hidden_k, update, preferred_element_type=jnp.float32
    )
    back = jnp.einsum(
        "pktd,prd->pktr", update, selected_up, preferred_element_type=jnp.float32
    ).astype(jnp.bfloat16)
    down_gradient_k = jnp.einsum(
        "pktr,pktd->pkrd", back, latents, preferred_element_type=jnp.float32
    )
    pairwise_up = ADAPTER_SCALE * jnp.sum(coefficient[:, :, None, None] * up_gradient_k, axis=1)
    pairwise_down = ADAPTER_SCALE * jnp.sum(coefficient[:, :, None, None] * down_gradient_k, axis=1)

    grads = jnp.stack([pairwise_down, pairwise_up], axis=1).reshape(
        pair_local, 2, adapter_rank_width, dp_size, col_local
    )
    grads = grads.transpose(3, 0, 1, 2, 4)
    gathered = lax.all_to_all(grads, "dp", 0, 0, tiled=True).reshape(
        dp_size * pair_local, 2 * adapter_rank_width * col_local
    )
    dense = jnp.dot(onehot_all.T, gathered, precision=lax.Precision.HIGHEST)
    dense = lax.psum(dense, "fsdp").reshape(class_total, 2, adapter_rank_width, col_local)
    grad_down = dense[:, 0]
    grad_up = dense[:, 1]
    return (grad_down, grad_up, losses)


def solution(mesh):
    placed = (
        P("dp", None, "fsdp", None),
        P("dp", None, "fsdp", None),
        P("fsdp", None),
        P(None, None, "dp"),
        P(None, None, "dp"),
        P("dp"),
        P("dp"),
    )
    return jax.shard_map(
        local,
        mesh=mesh,
        in_specs=placed,
        out_specs=(P(None, None, "dp"), P(None, None, "dp"), P("dp")),
        check_vma=False,
    )
```

```python
import jax
import jax.numpy as jnp
from jax import lax
from jax.sharding import PartitionSpec as P

ADAPTER_SCALE = 0.5
BETA = 1.0
LOSS_SCALE = 64.0


def fsdp_sum(value, fsdp_size):
    if fsdp_size != 4:
        return lax.psum(value, "fsdp")
    value = value + lax.ppermute(value, "fsdp", [(0, 1), (1, 0), (2, 3), (3, 2)])
    return value + lax.ppermute(value, "fsdp", [(0, 3), (3, 0), (1, 2), (2, 1)])


def local(latents, targets, frozen_weight, adapter_down, adapter_up, categories, timesteps):
    pair_local, _, row_local, feat_width = latents.shape
    class_total, adapter_rank_width, col_local = adapter_down.shape
    fsdp_size = lax.axis_size("fsdp")
    dp_size = lax.axis_size("dp")
    in_local = frozen_weight.shape[0]
    sample_rows = row_local * fsdp_size

    cats_all = lax.all_gather(categories, "dp", tiled=True)
    onehot_all = (cats_all[:, None] == jnp.arange(class_total, dtype=jnp.int32)[None, :]).astype(
        jnp.float32
    )
    counts = jnp.sum(onehot_all, axis=0)

    both = jnp.stack([adapter_down, adapter_up], axis=1)
    send = jnp.take(both, cats_all.reshape(dp_size, pair_local), axis=0)
    send, latents = lax.optimization_barrier((send, latents))
    recv = lax.all_to_all(send, "dp", 0, 0, tiled=True)
    selected = recv.transpose(1, 2, 3, 0, 4).reshape(
        pair_local, 2, adapter_rank_width, dp_size * col_local
    )
    selected_down = selected[:, 0]
    selected_up = selected[:, 1]

    x_split = latents.reshape(pair_local, 2, row_local, fsdp_size, in_local).transpose(3, 0, 1, 2, 4)
    x_slice = lax.all_to_all(x_split, "fsdp", 0, 0, tiled=True)
    partial = jnp.dot(
        x_slice.reshape(fsdp_size * pair_local * 2 * row_local, in_local),
        frozen_weight,
        preferred_element_type=jnp.float32,
    ).reshape(fsdp_size, pair_local * 2 * row_local, feat_width)
    base_out = lax.psum_scatter(
        partial.astype(jnp.bfloat16), "fsdp", scatter_dimension=0, tiled=True
    ).astype(jnp.float32).reshape(pair_local, 2, row_local, feat_width)

    grouped = latents.reshape(pair_local, 2 * row_local, feat_width)
    hidden_state = jnp.einsum(
        "psd,prd->psr", grouped, selected_down, preferred_element_type=jnp.float32
    ).astype(jnp.bfloat16)
    weight_change = ADAPTER_SCALE * jnp.einsum(
        "psr,prd->psd", hidden_state, selected_up, preferred_element_type=jnp.float32
    )
    weight_change = weight_change.reshape(pair_local, 2, row_local, feat_width)
    resid = base_out - targets.astype(jnp.float32)
    partial_err = jnp.sum(weight_change * (2.0 * resid + weight_change), axis=(2, 3))
    onehot = (categories[:, None] == jnp.arange(class_total, dtype=jnp.int32)[None, :]).astype(
        jnp.float32
    )
    errdiff = lax.psum(partial_err, "fsdp") / sample_rows
    kappa = BETA * (0.5 + timesteps.astype(jnp.float32) / 1000.0)
    zvalue = kappa * (errdiff[:, 0] - errdiff[:, 1])
    losses = jax.nn.softplus(zvalue)
    pair_total = jnp.sum(onehot * counts[None, :], axis=1)
    coef_pair = LOSS_SCALE * kappa * jax.nn.sigmoid(zvalue) / pair_total
    signs = jnp.array([2.0, -2.0], dtype=jnp.float32)
    coefficient = coef_pair[:, None] * signs[None, :] / sample_rows
    update = (resid + weight_change).astype(jnp.bfloat16)
    hidden_k = hidden_state.reshape(pair_local, 2, row_local, adapter_rank_width)
    up_gradient_k = jnp.einsum(
        "pktr,pktd->pkrd", hidden_k, update, preferred_element_type=jnp.float32
    )
    back = jnp.einsum(
        "pktd,prd->pktr", update, selected_up, preferred_element_type=jnp.float32
    ).astype(jnp.bfloat16)
    down_gradient_k = jnp.einsum(
        "pktr,pktd->pkrd", back, latents, preferred_element_type=jnp.float32
    )
    pairwise_up = ADAPTER_SCALE * jnp.sum(coefficient[:, :, None, None] * up_gradient_k, axis=1)
    pairwise_down = ADAPTER_SCALE * jnp.sum(coefficient[:, :, None, None] * down_gradient_k, axis=1)

    grads = jnp.stack([pairwise_down, pairwise_up], axis=1).reshape(
        pair_local, 2, adapter_rank_width, dp_size, col_local
    )
    grads = grads.transpose(3, 0, 1, 2, 4)
    gathered = lax.all_to_all(grads, "dp", 0, 0, tiled=True).reshape(
        dp_size * pair_local, 2 * adapter_rank_width * col_local
    )
    dense = jnp.dot(onehot_all.T, gathered, precision=lax.Precision.HIGHEST)
    dense = fsdp_sum(dense, fsdp_size).reshape(class_total, 2, adapter_rank_width, col_local)
    grad_down = dense[:, 0]
    grad_up = dense[:, 1]
    return (grad_down, grad_up, losses)


def solution(mesh):
    placed = (
        P("dp", None, "fsdp", None),
        P("dp", None, "fsdp", None),
        P("fsdp", None),
        P(None, None, "dp"),
        P(None, None, "dp"),
        P("dp"),
        P("dp"),
    )
    return jax.shard_map(
        local,
        mesh=mesh,
        in_specs=placed,
        out_specs=(P(None, None, "dp"), P(None, None, "dp"), P("dp")),
        check_vma=False,
    )
```

```python
import jax
import jax.numpy as jnp
from jax import lax
from jax.sharding import PartitionSpec as P

ADAPTER_SCALE = 0.5
BETA = 1.0
LOSS_SCALE = 64.0


def fsdp_sum(value, fsdp_size):
    if fsdp_size != 4:
        return lax.psum(value, "fsdp")
    value = value + lax.ppermute(value, "fsdp", [(0, 1), (1, 0), (2, 3), (3, 2)])
    return value + lax.ppermute(value, "fsdp", [(0, 3), (3, 0), (1, 2), (2, 1)])


def local(latents, targets, frozen_weight, adapter_down, adapter_up, categories, timesteps):
    pair_local, _, row_local, feat_width = latents.shape
    class_total, adapter_rank_width, col_local = adapter_down.shape
    fsdp_size = lax.axis_size("fsdp")
    dp_size = lax.axis_size("dp")
    in_local = frozen_weight.shape[0]
    sample_rows = row_local * fsdp_size

    cats_all = lax.all_gather(categories, "dp", tiled=True)
    onehot_all = (cats_all[:, None] == jnp.arange(class_total, dtype=jnp.int32)[None, :]).astype(
        jnp.float32
    )
    counts = jnp.sum(onehot_all, axis=0)

    both = jnp.stack([adapter_down, adapter_up], axis=1)
    send = jnp.take(both, cats_all.reshape(dp_size, pair_local), axis=0)
    send, latents = lax.optimization_barrier((send, latents))
    recv = lax.all_to_all(send, "dp", 0, 0, tiled=True)
    selected = recv.transpose(1, 2, 3, 0, 4).reshape(
        pair_local, 2, adapter_rank_width, dp_size * col_local
    )
    selected_down = selected[:, 0]
    selected_up = selected[:, 1]

    x_split = latents.reshape(pair_local, 2, row_local, fsdp_size, in_local).transpose(3, 0, 1, 2, 4)
    x_slice = lax.all_to_all(x_split, "fsdp", 0, 0, tiled=True)
    partial = jnp.dot(
        x_slice.reshape(fsdp_size * pair_local * 2 * row_local, in_local),
        frozen_weight,
        preferred_element_type=jnp.float32,
    ).reshape(fsdp_size, pair_local * 2 * row_local, feat_width)
    base_out = lax.psum_scatter(partial, "fsdp", scatter_dimension=0, tiled=True).reshape(
        pair_local, 2, row_local, feat_width
    )

    grouped = latents.reshape(pair_local, 2 * row_local, feat_width)
    hidden_state = jnp.einsum(
        "psd,prd->psr", grouped, selected_down, preferred_element_type=jnp.float32
    ).astype(jnp.bfloat16)
    weight_change = ADAPTER_SCALE * jnp.einsum(
        "psr,prd->psd", hidden_state, selected_up, preferred_element_type=jnp.float32
    )
    weight_change = weight_change.reshape(pair_local, 2, row_local, feat_width)
    resid = base_out - targets.astype(jnp.float32)
    partial_err = jnp.sum(weight_change * (2.0 * resid + weight_change), axis=(2, 3))
    onehot = (categories[:, None] == jnp.arange(class_total, dtype=jnp.int32)[None, :]).astype(
        jnp.float32
    )
    errdiff = lax.psum(partial_err, "fsdp") / sample_rows
    kappa = BETA * (0.5 + timesteps.astype(jnp.float32) / 1000.0)
    zvalue = kappa * (errdiff[:, 0] - errdiff[:, 1])
    losses = jax.nn.softplus(zvalue)
    pair_total = jnp.sum(onehot * counts[None, :], axis=1)
    coef_pair = LOSS_SCALE * kappa * jax.nn.sigmoid(zvalue) / pair_total
    signs = jnp.array([2.0, -2.0], dtype=jnp.float32)
    coefficient = coef_pair[:, None] * signs[None, :] / sample_rows
    update = (resid + weight_change).astype(jnp.bfloat16)
    hidden_k = hidden_state.reshape(pair_local, 2, row_local, adapter_rank_width)
    up_gradient_k = jnp.einsum(
        "pktr,pktd->pkrd", hidden_k, update, preferred_element_type=jnp.float32
    )
    back = jnp.einsum(
        "pktd,prd->pktr", update, selected_up, preferred_element_type=jnp.float32
    ).astype(jnp.bfloat16)
    down_gradient_k = jnp.einsum(
        "pktr,pktd->pkrd", back, latents, preferred_element_type=jnp.float32
    )
    pairwise_up = ADAPTER_SCALE * jnp.sum(coefficient[:, :, None, None] * up_gradient_k, axis=1)
    pairwise_down = ADAPTER_SCALE * jnp.sum(coefficient[:, :, None, None] * down_gradient_k, axis=1)

    grads = jnp.stack([pairwise_down, pairwise_up], axis=1).reshape(
        pair_local, 2, adapter_rank_width, dp_size, col_local
    )
    grads = grads.transpose(3, 0, 1, 2, 4)
    gathered = lax.all_to_all(grads, "dp", 0, 0, tiled=True).reshape(
        dp_size * pair_local, 2 * adapter_rank_width * col_local
    )
    dense = jnp.dot(onehot_all.T, gathered, precision=lax.Precision.HIGHEST)
    dense = fsdp_sum(dense, fsdp_size).reshape(class_total, 2, adapter_rank_width, col_local)
    grad_down = dense[:, 0]
    grad_up = dense[:, 1]
    return (grad_down, grad_up, losses)


def solution(mesh):
    placed = (
        P("dp", None, "fsdp", None),
        P("dp", None, "fsdp", None),
        P("fsdp", None),
        P(None, None, "dp"),
        P(None, None, "dp"),
        P("dp"),
        P("dp"),
    )
    return jax.shard_map(
        local,
        mesh=mesh,
        in_specs=placed,
        out_specs=(P(None, None, "dp"), P(None, None, "dp"), P("dp")),
        check_vma=False,
    )
```

```python
import jax
import jax.numpy as jnp
from jax import lax
from jax.sharding import PartitionSpec as P

ADAPTER_SCALE = 0.5
BETA = 1.0
LOSS_SCALE = 64.0


def fsdp_sum(value, fsdp_size):
    if fsdp_size != 4:
        return lax.psum(value, "fsdp")
    value = value + lax.ppermute(value, "fsdp", [(0, 1), (1, 0), (2, 3), (3, 2)])
    return value + lax.ppermute(value, "fsdp", [(0, 3), (3, 0), (1, 2), (2, 1)])


def local(latents, targets, frozen_weight, adapter_down, adapter_up, categories, timesteps):
    pair_local, _, row_local, feat_width = latents.shape
    class_total, adapter_rank_width, col_local = adapter_down.shape
    fsdp_size = lax.axis_size("fsdp")
    dp_size = lax.axis_size("dp")
    in_local = frozen_weight.shape[0]
    sample_rows = row_local * fsdp_size

    cats_all = lax.all_gather(categories, "dp", tiled=True)
    onehot_all = (cats_all[:, None] == jnp.arange(class_total, dtype=jnp.int32)[None, :]).astype(
        jnp.float32
    )
    counts = jnp.sum(onehot_all, axis=0)

    both = jnp.stack([adapter_down, adapter_up], axis=1)
    send = jnp.take(both, cats_all.reshape(dp_size, pair_local), axis=0)
    recv = lax.all_to_all(send, "dp", 0, 0, tiled=True)
    selected = recv.transpose(1, 2, 3, 0, 4).reshape(
        pair_local, 2, adapter_rank_width, dp_size * col_local
    )
    selected_down = selected[:, 0]
    selected_up = selected[:, 1]

    highest = lax.Precision.HIGHEST
    hidden_state = jnp.einsum(
        "pktd,prd->pktr", latents, selected_down, preferred_element_type=jnp.float32
    ).astype(jnp.bfloat16)
    hidden_f = hidden_state.astype(jnp.float32)
    v_block = jnp.einsum(
        "prd,ed->pre", selected_up, frozen_weight, preferred_element_type=jnp.float32
    )
    v_full = lax.all_gather(v_block, "fsdp", axis=2, tiled=True)
    a_k = jnp.einsum(
        "pktr,pktd->pkrd", hidden_state, latents, preferred_element_type=jnp.float32
    ).reshape(pair_local, 2, adapter_rank_width, fsdp_size, in_local)
    a_k = lax.psum_scatter(
        a_k.transpose(3, 0, 1, 2, 4), "fsdp", scatter_dimension=0, tiled=True
    ).reshape(pair_local, 2, adapter_rank_width, in_local)
    base_up = jnp.einsum("pktd,prd->pktr", latents, v_full, precision=highest)
    target_up = jnp.einsum(
        "pktd,prd->pktr", targets, selected_up, preferred_element_type=jnp.float32
    )
    up_gram = jnp.einsum(
        "prd,pqd->prq", selected_up, selected_up, preferred_element_type=jnp.float32
    )
    delta_up = ADAPTER_SCALE * jnp.einsum("pktr,prq->pktq", hidden_f, up_gram, precision=highest)
    partial_err = jnp.sum(
        hidden_f * (base_up - target_up + 0.5 * delta_up), axis=(2, 3)
    ) * (2.0 * ADAPTER_SCALE)
    back = base_up - target_up + delta_up

    onehot = (categories[:, None] == jnp.arange(class_total, dtype=jnp.int32)[None, :]).astype(
        jnp.float32
    )
    errdiff = lax.psum(partial_err, "fsdp") / sample_rows
    kappa = BETA * (0.5 + timesteps.astype(jnp.float32) / 1000.0)
    zvalue = kappa * (errdiff[:, 0] - errdiff[:, 1])
    losses = jax.nn.softplus(zvalue)
    pair_total = jnp.sum(onehot * counts[None, :], axis=1)
    coef_pair = LOSS_SCALE * kappa * jax.nn.sigmoid(zvalue) / pair_total
    signs = jnp.array([2.0, -2.0], dtype=jnp.float32)
    coefficient = coef_pair[:, None] * signs[None, :] / sample_rows

    hidden_gram = jnp.einsum(
        "pktr,pktq->pkrq", hidden_state, hidden_state, preferred_element_type=jnp.float32
    )
    up_gradient_k = (
        jnp.einsum("pkre,ed->pkrd", a_k, frozen_weight, precision=highest)
        - jnp.einsum("pktr,pktd->pkrd", hidden_state, targets, preferred_element_type=jnp.float32)
        + ADAPTER_SCALE * jnp.einsum("pkrq,pqd->pkrd", hidden_gram, selected_up, precision=highest)
    )
    down_gradient_k = jnp.einsum("pktr,pktd->pkrd", back, latents, precision=highest)
    pairwise_up = ADAPTER_SCALE * jnp.sum(coefficient[:, :, None, None] * up_gradient_k, axis=1)
    pairwise_down = ADAPTER_SCALE * jnp.sum(coefficient[:, :, None, None] * down_gradient_k, axis=1)

    grads = jnp.stack([pairwise_down, pairwise_up], axis=1).reshape(
        pair_local, 2, adapter_rank_width, dp_size, col_local
    )
    grads = grads.transpose(3, 0, 1, 2, 4)
    gathered = lax.all_to_all(grads, "dp", 0, 0, tiled=True).reshape(
        dp_size * pair_local, 2 * adapter_rank_width * col_local
    )
    dense = jnp.dot(onehot_all.T, gathered, precision=lax.Precision.HIGHEST)
    dense = fsdp_sum(dense, fsdp_size).reshape(class_total, 2, adapter_rank_width, col_local)
    grad_down = dense[:, 0]
    grad_up = dense[:, 1]
    return (grad_down, grad_up, losses)


def solution(mesh):
    placed = (
        P("dp", None, "fsdp", None),
        P("dp", None, "fsdp", None),
        P("fsdp", None),
        P(None, None, "dp"),
        P(None, None, "dp"),
        P("dp"),
        P("dp"),
    )
    return jax.shard_map(
        local,
        mesh=mesh,
        in_specs=placed,
        out_specs=(P(None, None, "dp"), P(None, None, "dp"), P("dp")),
        check_vma=False,
    )
```

```python
import jax
import jax.numpy as jnp
from jax import lax
from jax.sharding import PartitionSpec as P

ADAPTER_SCALE = 0.5
BETA = 1.0
LOSS_SCALE = 64.0


def fsdp_sum(value, fsdp_size):
    if fsdp_size != 4:
        return lax.psum(value, "fsdp")
    value = value + lax.ppermute(value, "fsdp", [(0, 1), (1, 0), (2, 3), (3, 2)])
    return value + lax.ppermute(value, "fsdp", [(0, 3), (3, 0), (1, 2), (2, 1)])


def local(latents, targets, frozen_weight, adapter_down, adapter_up, categories, timesteps):
    pair_local, _, row_local, feat_width = latents.shape
    class_total, adapter_rank_width, col_local = adapter_down.shape
    fsdp_size = lax.axis_size("fsdp")
    dp_size = lax.axis_size("dp")
    in_local = frozen_weight.shape[0]
    sample_rows = row_local * fsdp_size

    cats_all = lax.all_gather(categories, "dp", tiled=True)
    onehot_all = (cats_all[:, None] == jnp.arange(class_total, dtype=jnp.int32)[None, :]).astype(
        jnp.float32
    )
    counts = jnp.sum(onehot_all, axis=0)

    both = jnp.stack([adapter_down, adapter_up], axis=1)
    send = jnp.take(both, cats_all.reshape(dp_size, pair_local), axis=0)
    recv = lax.all_to_all(send, "dp", 0, 0, tiled=True)
    selected = recv.transpose(1, 2, 3, 0, 4).reshape(
        pair_local, 2, adapter_rank_width, dp_size * col_local
    )
    selected_down = selected[:, 0]
    selected_up = selected[:, 1]

    highest = lax.Precision.HIGHEST
    hidden_state = jnp.einsum(
        "pktd,prd->pktr", latents, selected_down, preferred_element_type=jnp.float32
    ).astype(jnp.bfloat16)
    hidden_f = hidden_state.astype(jnp.float32)
    v_block = jnp.einsum(
        "prd,ed->pre", selected_up, frozen_weight, preferred_element_type=jnp.float32
    )
    v_full = lax.all_gather(v_block, "fsdp", axis=2, tiled=True)
    a_k = jnp.einsum(
        "pktr,pktd->pkrd", hidden_state, latents, preferred_element_type=jnp.float32
    ).reshape(pair_local, 2, adapter_rank_width, fsdp_size, in_local)
    a_k = lax.psum_scatter(
        a_k.transpose(3, 0, 1, 2, 4), "fsdp", scatter_dimension=0, tiled=True
    ).reshape(pair_local, 2, adapter_rank_width, in_local)
    base_up = jnp.einsum("pktd,prd->pktr", latents, v_full, precision=highest)
    target_up = jnp.einsum(
        "pktd,prd->pktr", targets, selected_up, preferred_element_type=jnp.float32
    )
    up_gram = jnp.einsum(
        "prd,pqd->prq", selected_up, selected_up, preferred_element_type=jnp.float32
    )
    delta_up = ADAPTER_SCALE * jnp.einsum("pktr,prq->pktq", hidden_f, up_gram, precision=highest)
    partial_err = jnp.sum(
        hidden_f * (base_up - target_up + 0.5 * delta_up), axis=(2, 3)
    ) * (2.0 * ADAPTER_SCALE)
    back = base_up - target_up + delta_up

    onehot = (categories[:, None] == jnp.arange(class_total, dtype=jnp.int32)[None, :]).astype(
        jnp.float32
    )
    errdiff = lax.psum(partial_err, "fsdp") / sample_rows
    kappa = BETA * (0.5 + timesteps.astype(jnp.float32) / 1000.0)
    zvalue = kappa * (errdiff[:, 0] - errdiff[:, 1])
    losses = jax.nn.softplus(zvalue)
    pair_total = jnp.sum(onehot * counts[None, :], axis=1)
    coef_pair = LOSS_SCALE * kappa * jax.nn.sigmoid(zvalue) / pair_total
    signs = jnp.array([2.0, -2.0], dtype=jnp.float32)
    coefficient = coef_pair[:, None] * signs[None, :] / sample_rows

    scale_k = (ADAPTER_SCALE * coefficient)[:, :, None, None]
    hidden_gram = jnp.einsum(
        "pktr,pktq->pkrq", hidden_state, hidden_state, preferred_element_type=jnp.float32
    )
    a_weighted = jnp.sum(scale_k * a_k, axis=1)
    gram_weighted = ADAPTER_SCALE * jnp.sum(scale_k * hidden_gram, axis=1)
    up_t = (
        jnp.einsum("ed,pre->pdr", frozen_weight, a_weighted, precision=highest)
        - jnp.einsum("pktd,pktr->pdr", targets, hidden_f * scale_k, precision=highest)
        + jnp.einsum("pqd,prq->pdr", selected_up, gram_weighted, precision=highest)
    )
    down_t = jnp.einsum("pktd,pktr->pdr", latents, back * scale_k, precision=highest)
    grads = jnp.concatenate([down_t, up_t], axis=2).reshape(
        pair_local, dp_size, col_local, 2 * adapter_rank_width
    )

    gathered = lax.all_to_all(grads.transpose(1, 0, 2, 3), "dp", 0, 0, tiled=True).reshape(
        dp_size * pair_local, col_local * 2 * adapter_rank_width
    )
    dense = jnp.dot(onehot_all.T, gathered, precision=lax.Precision.HIGHEST)
    dense = fsdp_sum(dense, fsdp_size).reshape(class_total, col_local, 2, adapter_rank_width)
    grad_down = dense[:, :, 0].transpose(0, 2, 1)
    grad_up = dense[:, :, 1].transpose(0, 2, 1)
    return (grad_down, grad_up, losses)


def solution(mesh):
    placed = (
        P("dp", None, "fsdp", None),
        P("dp", None, "fsdp", None),
        P("fsdp", None),
        P(None, None, "dp"),
        P(None, None, "dp"),
        P("dp"),
        P("dp"),
    )
    return jax.shard_map(
        local,
        mesh=mesh,
        in_specs=placed,
        out_specs=(P(None, None, "dp"), P(None, None, "dp"), P("dp")),
        check_vma=False,
    )
```

```python
import jax
import jax.numpy as jnp
from jax import lax
from jax.sharding import PartitionSpec as P

ADAPTER_SCALE = 0.5
BETA = 1.0
LOSS_SCALE = 64.0


def fsdp_sum(value, fsdp_size):
    if fsdp_size != 4:
        return lax.psum(value, "fsdp")
    value = value + lax.ppermute(value, "fsdp", [(0, 1), (1, 0), (2, 3), (3, 2)])
    return value + lax.ppermute(value, "fsdp", [(0, 3), (3, 0), (1, 2), (2, 1)])


def local(latents, targets, frozen_weight, adapter_down, adapter_up, categories, timesteps):
    pair_local, _, row_local, feat_width = latents.shape
    class_total, adapter_rank_width, col_local = adapter_down.shape
    fsdp_size = lax.axis_size("fsdp")
    dp_size = lax.axis_size("dp")
    in_local = frozen_weight.shape[0]
    sample_rows = row_local * fsdp_size

    cats_all = lax.all_gather(categories, "dp", tiled=True)
    onehot_all = (cats_all[:, None] == jnp.arange(class_total, dtype=jnp.int32)[None, :]).astype(
        jnp.float32
    )
    counts = jnp.sum(onehot_all, axis=0)

    both = jnp.stack([adapter_down, adapter_up], axis=1).transpose(0, 3, 1, 2)
    send = jnp.take(both, cats_all.reshape(dp_size, pair_local), axis=0)
    recv = lax.all_to_all(send, "dp", 0, 0, tiled=True)
    selected = recv.transpose(1, 0, 2, 3, 4).reshape(
        pair_local, dp_size * col_local, 2, adapter_rank_width
    )
    down_t = selected[:, :, 0]
    up_t = selected[:, :, 1]

    highest = lax.Precision.HIGHEST
    hidden_state = jnp.einsum(
        "pktd,pdr->pktr", latents, down_t, preferred_element_type=jnp.float32
    ).astype(jnp.bfloat16)
    hidden_f = hidden_state.astype(jnp.float32)
    v_block = jnp.einsum("ed,pdr->per", frozen_weight, up_t, preferred_element_type=jnp.float32)
    shifted = [v_block] + [
        lax.ppermute(
            v_block, "fsdp", [((dst + shift) % fsdp_size, dst) for dst in range(fsdp_size)]
        )
        for shift in range(1, fsdp_size)
    ]
    stacked = jnp.stack(shifted + shifted, axis=0)
    own = lax.axis_index("fsdp")
    v_by_source = lax.dynamic_slice_in_dim(stacked, (fsdp_size - own) % fsdp_size, fsdp_size, 0)
    latents_blocks = latents.reshape(pair_local, 2, row_local, fsdp_size, in_local)
    a_k = jnp.einsum(
        "pktr,pktd->pkrd", hidden_state, latents, preferred_element_type=jnp.float32
    ).reshape(pair_local, 2, adapter_rank_width, fsdp_size, in_local)
    a_k = lax.psum_scatter(
        a_k.transpose(3, 0, 1, 2, 4), "fsdp", scatter_dimension=0, tiled=True
    ).reshape(pair_local, 2, adapter_rank_width, in_local)
    target_up = jnp.einsum(
        "pktd,pdr->pktr", targets, up_t, preferred_element_type=jnp.float32
    )
    up_gram = jnp.einsum("pdr,pdq->prq", up_t, up_t, preferred_element_type=jnp.float32)
    delta_up = ADAPTER_SCALE * jnp.einsum("pktr,prq->pktq", hidden_f, up_gram, precision=highest)
    base_term = jnp.sum(a_k * v_block[:, None].transpose(0, 1, 3, 2), axis=(2, 3))
    partial_err = (
        jnp.sum(hidden_f * (0.5 * delta_up - target_up), axis=(2, 3)) + base_term
    ) * (2.0 * ADAPTER_SCALE)
    base_up = jnp.einsum("pktfe,fper->pktr", latents_blocks, v_by_source, precision=highest)
    back = base_up - target_up + delta_up

    onehot = (categories[:, None] == jnp.arange(class_total, dtype=jnp.int32)[None, :]).astype(
        jnp.float32
    )
    errdiff = lax.psum(partial_err, "fsdp") / sample_rows
    kappa = BETA * (0.5 + timesteps.astype(jnp.float32) / 1000.0)
    zvalue = kappa * (errdiff[:, 0] - errdiff[:, 1])
    losses = jax.nn.softplus(zvalue)
    pair_total = jnp.sum(onehot * counts[None, :], axis=1)
    coef_pair = LOSS_SCALE * kappa * jax.nn.sigmoid(zvalue) / pair_total
    signs = jnp.array([2.0, -2.0], dtype=jnp.float32)
    coefficient = coef_pair[:, None] * signs[None, :] / sample_rows

    scale_k = (ADAPTER_SCALE * coefficient)[:, :, None, None]
    hidden_gram = jnp.einsum(
        "pktr,pktq->pkrq", hidden_state, hidden_state, preferred_element_type=jnp.float32
    )
    a_weighted = jnp.sum(scale_k * a_k, axis=1)
    gram_weighted = ADAPTER_SCALE * jnp.sum(scale_k * hidden_gram, axis=1)
    up_t = (
        jnp.einsum("ed,pre->pdr", frozen_weight, a_weighted, precision=highest)
        - jnp.einsum("pktd,pktr->pdr", targets, hidden_f * scale_k, precision=highest)
        + jnp.einsum("pdq,prq->pdr", up_t, gram_weighted, precision=highest)
    )
    down_t = jnp.einsum("pktd,pktr->pdr", latents, back * scale_k, precision=highest)
    grads = jnp.concatenate([down_t, up_t], axis=2).reshape(
        pair_local, dp_size, col_local, 2 * adapter_rank_width
    )

    gathered = lax.all_to_all(grads.transpose(1, 0, 2, 3), "dp", 0, 0, tiled=True).reshape(
        dp_size * pair_local, col_local * 2 * adapter_rank_width
    )
    dense = jnp.dot(onehot_all.T, gathered, precision=lax.Precision.HIGHEST)
    dense = fsdp_sum(dense, fsdp_size).reshape(class_total, col_local, 2, adapter_rank_width)
    grad_down = dense[:, :, 0].transpose(0, 2, 1)
    grad_up = dense[:, :, 1].transpose(0, 2, 1)
    return (grad_down, grad_up, losses)


def solution(mesh):
    placed = (
        P("dp", None, "fsdp", None),
        P("dp", None, "fsdp", None),
        P("fsdp", None),
        P(None, None, "dp"),
        P(None, None, "dp"),
        P("dp"),
        P("dp"),
    )
    return jax.shard_map(
        local,
        mesh=mesh,
        in_specs=placed,
        out_specs=(P(None, None, "dp"), P(None, None, "dp"), P("dp")),
        check_vma=False,
    )
```

```python
import jax
import jax.numpy as jnp
from jax import lax
from jax.sharding import PartitionSpec as P

ADAPTER_SCALE = 0.5
BETA = 1.0
LOSS_SCALE = 64.0


def fsdp_sum(value, fsdp_size):
    if fsdp_size != 4:
        return lax.psum(value, "fsdp")
    value = value + lax.ppermute(value, "fsdp", [(0, 1), (1, 0), (2, 3), (3, 2)])
    return value + lax.ppermute(value, "fsdp", [(0, 3), (3, 0), (1, 2), (2, 1)])


def local(latents, targets, frozen_weight, adapter_down, adapter_up, categories, timesteps):
    pair_local, _, row_local, feat_width = latents.shape
    class_total, adapter_rank_width, col_local = adapter_down.shape
    fsdp_size = lax.axis_size("fsdp")
    dp_size = lax.axis_size("dp")
    in_local = frozen_weight.shape[0]
    sample_rows = row_local * fsdp_size

    cats_all = lax.all_gather(categories, "dp", tiled=True)
    onehot_all = (cats_all[:, None] == jnp.arange(class_total, dtype=jnp.int32)[None, :]).astype(
        jnp.float32
    )
    counts = jnp.sum(onehot_all, axis=0)

    both = jnp.stack(
        [adapter_down.transpose(0, 2, 1), adapter_up.transpose(0, 2, 1)], axis=2
    ).reshape(class_total, col_local * 2 * adapter_rank_width)
    send = jnp.dot(
        onehot_all.astype(jnp.bfloat16), both, preferred_element_type=jnp.float32
    ).astype(jnp.bfloat16)
    recv = lax.all_to_all(
        send.reshape(dp_size, pair_local, col_local * 2 * adapter_rank_width), "dp", 0, 0, tiled=True
    )
    selected = recv.reshape(dp_size, pair_local, col_local, 2, adapter_rank_width).transpose(
        1, 0, 2, 3, 4
    ).reshape(pair_local, dp_size * col_local, 2, adapter_rank_width)
    down_t = selected[:, :, 0]
    up_t = selected[:, :, 1]

    highest = lax.Precision.HIGHEST
    hidden_state = jnp.einsum(
        "pktd,pdr->pktr", latents, down_t, preferred_element_type=jnp.float32
    ).astype(jnp.bfloat16)
    hidden_f = hidden_state.astype(jnp.float32)
    v_block = jnp.einsum(
        "pdr,ed->pre", up_t, frozen_weight, preferred_element_type=jnp.float32
    )
    v_full = lax.all_gather(v_block, "fsdp", axis=2, tiled=True)
    a_k = jnp.einsum(
        "pktr,pktd->pkrd", hidden_state, latents, preferred_element_type=jnp.float32
    ).reshape(pair_local, 2, adapter_rank_width, fsdp_size, in_local)
    a_k = lax.psum_scatter(
        a_k.transpose(3, 0, 1, 2, 4), "fsdp", scatter_dimension=0, tiled=True
    ).reshape(pair_local, 2, adapter_rank_width, in_local)
    base_up = jnp.einsum("pktd,prd->pktr", latents, v_full, precision=highest)
    target_up = jnp.einsum(
        "pktd,pdr->pktr", targets, up_t, preferred_element_type=jnp.float32
    )
    up_gram = jnp.einsum(
        "pdr,pdq->prq", up_t, up_t, preferred_element_type=jnp.float32
    )
    delta_up = ADAPTER_SCALE * jnp.einsum("pktr,prq->pktq", hidden_f, up_gram, precision=highest)
    partial_err = jnp.sum(
        hidden_f * (base_up - target_up + 0.5 * delta_up), axis=(2, 3)
    ) * (2.0 * ADAPTER_SCALE)
    back = base_up - target_up + delta_up

    onehot = (categories[:, None] == jnp.arange(class_total, dtype=jnp.int32)[None, :]).astype(
        jnp.float32
    )
    errdiff = lax.psum(partial_err, "fsdp") / sample_rows
    kappa = BETA * (0.5 + timesteps.astype(jnp.float32) / 1000.0)
    zvalue = kappa * (errdiff[:, 0] - errdiff[:, 1])
    losses = jax.nn.softplus(zvalue)
    pair_total = jnp.sum(onehot * counts[None, :], axis=1)
    coef_pair = LOSS_SCALE * kappa * jax.nn.sigmoid(zvalue) / pair_total
    signs = jnp.array([2.0, -2.0], dtype=jnp.float32)
    coefficient = coef_pair[:, None] * signs[None, :] / sample_rows

    scale_k = (ADAPTER_SCALE * coefficient)[:, :, None, None]
    hidden_gram = jnp.einsum(
        "pktr,pktq->pkrq", hidden_state, hidden_state, preferred_element_type=jnp.float32
    )
    a_weighted = jnp.sum(scale_k * a_k, axis=1)
    gram_weighted = ADAPTER_SCALE * jnp.sum(scale_k * hidden_gram, axis=1)
    up_t = (
        jnp.einsum("ed,pre->pdr", frozen_weight, a_weighted, precision=highest)
        - jnp.einsum("pktd,pktr->pdr", targets, hidden_f * scale_k, precision=highest)
        + jnp.einsum("pdq,prq->pdr", up_t, gram_weighted, precision=highest)
    )
    down_t = jnp.einsum("pktd,pktr->pdr", latents, back * scale_k, precision=highest)
    grads = jnp.concatenate([down_t, up_t], axis=2).reshape(
        pair_local, dp_size, col_local, 2 * adapter_rank_width
    )

    gathered = lax.all_to_all(grads.transpose(1, 0, 2, 3), "dp", 0, 0, tiled=True).reshape(
        dp_size * pair_local, col_local * 2 * adapter_rank_width
    )
    dense = jnp.dot(onehot_all.T, gathered, precision=lax.Precision.HIGHEST)
    dense = fsdp_sum(dense, fsdp_size).reshape(class_total, col_local, 2, adapter_rank_width)
    grad_down = dense[:, :, 0].transpose(0, 2, 1)
    grad_up = dense[:, :, 1].transpose(0, 2, 1)
    return (grad_down, grad_up, losses)


def solution(mesh):
    placed = (
        P("dp", None, "fsdp", None),
        P("dp", None, "fsdp", None),
        P("fsdp", None),
        P(None, None, "dp"),
        P(None, None, "dp"),
        P("dp"),
        P("dp"),
    )
    return jax.shard_map(
        local,
        mesh=mesh,
        in_specs=placed,
        out_specs=(P(None, None, "dp"), P(None, None, "dp"), P("dp")),
        check_vma=False,
    )
```

```python
import jax
import jax.numpy as jnp
from jax import lax
from jax.sharding import PartitionSpec as P

ADAPTER_SCALE = 0.5
BETA = 1.0
LOSS_SCALE = 64.0


def fsdp_sum(value, fsdp_size):
    if fsdp_size != 4:
        return lax.psum(value, "fsdp")
    value = value + lax.ppermute(value, "fsdp", [(0, 1), (1, 0), (2, 3), (3, 2)])
    return value + lax.ppermute(value, "fsdp", [(0, 3), (3, 0), (1, 2), (2, 1)])


def local(latents, targets, frozen_weight, adapter_down, adapter_up, categories, timesteps):
    pair_local, _, row_local, feat_width = latents.shape
    class_total, adapter_rank_width, col_local = adapter_down.shape
    fsdp_size = lax.axis_size("fsdp")
    dp_size = lax.axis_size("dp")
    in_local = frozen_weight.shape[0]
    sample_rows = row_local * fsdp_size

    cats_all = lax.all_gather(categories, "dp", tiled=True)
    onehot_all = (cats_all[:, None] == jnp.arange(class_total, dtype=jnp.int32)[None, :]).astype(
        jnp.float32
    )
    counts = jnp.sum(onehot_all, axis=0)

    both = jnp.stack([adapter_down, adapter_up], axis=1)
    send = jnp.take(both, cats_all.reshape(dp_size, pair_local), axis=0)
    recv = lax.all_to_all(send, "dp", 0, 0, tiled=True)
    selected = recv.transpose(1, 2, 3, 0, 4).reshape(
        pair_local, 2, adapter_rank_width, dp_size * col_local
    )
    selected_down = selected[:, 0]
    selected_up = selected[:, 1]

    highest = lax.Precision.HIGHEST
    hidden_state = jnp.einsum(
        "pktd,prd->pktr", latents, selected_down, preferred_element_type=jnp.float32
    ).astype(jnp.bfloat16)
    hidden_f = hidden_state.astype(jnp.float32)
    v_block = jnp.einsum(
        "prd,ed->pre", selected_up, frozen_weight, preferred_element_type=jnp.float32
    )
    v_full = lax.all_gather(v_block, "fsdp", axis=2, tiled=True)
    a_k = jnp.einsum(
        "pktr,pktd->pkrd", hidden_state, latents, preferred_element_type=jnp.float32
    ).reshape(pair_local, 2, adapter_rank_width, fsdp_size, in_local)
    a_k, v_full = lax.optimization_barrier((a_k, v_full))
    a_k = lax.psum_scatter(
        a_k.transpose(3, 0, 1, 2, 4), "fsdp", scatter_dimension=0, tiled=True
    ).reshape(pair_local, 2, adapter_rank_width, in_local)
    base_up = jnp.einsum("pktd,prd->pktr", latents, v_full, precision=highest)
    target_up = jnp.einsum(
        "pktd,prd->pktr", targets, selected_up, preferred_element_type=jnp.float32
    )
    up_gram = jnp.einsum(
        "prd,pqd->prq", selected_up, selected_up, preferred_element_type=jnp.float32
    )
    delta_up = ADAPTER_SCALE * jnp.einsum("pktr,prq->pktq", hidden_f, up_gram, precision=highest)
    partial_err = jnp.sum(
        hidden_f * (base_up - target_up + 0.5 * delta_up), axis=(2, 3)
    ) * (2.0 * ADAPTER_SCALE)
    back = base_up - target_up + delta_up

    onehot = (categories[:, None] == jnp.arange(class_total, dtype=jnp.int32)[None, :]).astype(
        jnp.float32
    )
    errdiff = lax.psum(partial_err, "fsdp") / sample_rows
    kappa = BETA * (0.5 + timesteps.astype(jnp.float32) / 1000.0)
    zvalue = kappa * (errdiff[:, 0] - errdiff[:, 1])
    losses = jax.nn.softplus(zvalue)
    pair_total = jnp.sum(onehot * counts[None, :], axis=1)
    coef_pair = LOSS_SCALE * kappa * jax.nn.sigmoid(zvalue) / pair_total
    signs = jnp.array([2.0, -2.0], dtype=jnp.float32)
    coefficient = coef_pair[:, None] * signs[None, :] / sample_rows

    scale_k = (ADAPTER_SCALE * coefficient)[:, :, None, None]
    hidden_gram = jnp.einsum(
        "pktr,pktq->pkrq", hidden_state, hidden_state, preferred_element_type=jnp.float32
    )
    a_weighted = jnp.sum(scale_k * a_k, axis=1)
    gram_weighted = ADAPTER_SCALE * jnp.sum(scale_k * hidden_gram, axis=1)
    up_t = (
        jnp.einsum("ed,pre->pdr", frozen_weight, a_weighted, precision=highest)
        - jnp.einsum("pktd,pktr->pdr", targets, hidden_f * scale_k, precision=highest)
        + jnp.einsum("pqd,prq->pdr", selected_up, gram_weighted, precision=highest)
    )
    down_t = jnp.einsum("pktd,pktr->pdr", latents, back * scale_k, precision=highest)
    grads = jnp.concatenate([down_t, up_t], axis=2).reshape(
        pair_local, dp_size, col_local, 2 * adapter_rank_width
    )

    gathered = lax.all_to_all(grads.transpose(1, 0, 2, 3), "dp", 0, 0, tiled=True).reshape(
        dp_size * pair_local, col_local * 2 * adapter_rank_width
    )
    dense = jnp.dot(onehot_all.T, gathered, precision=lax.Precision.HIGHEST)
    dense = fsdp_sum(dense, fsdp_size).reshape(class_total, col_local, 2, adapter_rank_width)
    grad_down = dense[:, :, 0].transpose(0, 2, 1)
    grad_up = dense[:, :, 1].transpose(0, 2, 1)
    return (grad_down, grad_up, losses)


def solution(mesh):
    placed = (
        P("dp", None, "fsdp", None),
        P("dp", None, "fsdp", None),
        P("fsdp", None),
        P(None, None, "dp"),
        P(None, None, "dp"),
        P("dp"),
        P("dp"),
    )
    return jax.shard_map(
        local,
        mesh=mesh,
        in_specs=placed,
        out_specs=(P(None, None, "dp"), P(None, None, "dp"), P("dp")),
        check_vma=False,
    )
```

```python
import jax
import jax.numpy as jnp
from jax import lax
from jax.sharding import PartitionSpec as P

ADAPTER_SCALE = 0.5
BETA = 1.0
LOSS_SCALE = 64.0


def fsdp_sum(value, fsdp_size):
    if fsdp_size != 4:
        return lax.psum(value, "fsdp")
    value = value + lax.ppermute(value, "fsdp", [(0, 1), (1, 0), (2, 3), (3, 2)])
    return value + lax.ppermute(value, "fsdp", [(0, 3), (3, 0), (1, 2), (2, 1)])


def local(latents, targets, frozen_weight, adapter_down, adapter_up, categories, timesteps):
    pair_local, _, row_local, feat_width = latents.shape
    class_total, adapter_rank_width, col_local = adapter_down.shape
    fsdp_size = lax.axis_size("fsdp")
    dp_size = lax.axis_size("dp")
    in_local = frozen_weight.shape[0]
    sample_rows = row_local * fsdp_size

    own = lax.axis_index("fsdp")
    shift_ids = jnp.arange(fsdp_size, dtype=jnp.int32)
    latents_split = latents.reshape(pair_local, 2, row_local, fsdp_size, in_local)
    blocks_by_shift = jnp.stack(
        [
            lax.ppermute(
                lax.dynamic_index_in_dim(
                    latents_split, (own + shift) % fsdp_size, axis=3, keepdims=False
                ),
                "fsdp",
                [(src, (src + shift) % fsdp_size) for src in range(fsdp_size)],
            )
            if shift
            else lax.dynamic_index_in_dim(latents_split, own, axis=3, keepdims=False)
            for shift in range(fsdp_size)
        ],
        axis=0,
    )

    cats_all = lax.all_gather(categories, "dp", tiled=True)
    onehot_all = (cats_all[:, None] == jnp.arange(class_total, dtype=jnp.int32)[None, :]).astype(
        jnp.float32
    )
    counts = jnp.sum(onehot_all, axis=0)

    both = jnp.stack([adapter_down, adapter_up], axis=1)
    send = jnp.take(both, cats_all.reshape(dp_size, pair_local), axis=0)
    recv = lax.all_to_all(send, "dp", 0, 0, tiled=True)
    selected = recv.transpose(1, 2, 3, 0, 4).reshape(
        pair_local, 2, adapter_rank_width, dp_size * col_local
    )
    selected_down = selected[:, 0]
    selected_up = selected[:, 1]

    highest = lax.Precision.HIGHEST
    hidden_state = jnp.einsum(
        "pktd,prd->pktr", latents, selected_down, preferred_element_type=jnp.float32
    ).astype(jnp.bfloat16)
    hidden_f = hidden_state.astype(jnp.float32)
    v_block = jnp.einsum(
        "prd,ed->pre", selected_up, frozen_weight, preferred_element_type=jnp.float32
    )
    hidden_cols = hidden_f.transpose(0, 3, 1, 2).reshape(pair_local, adapter_rank_width, 2 * row_local)
    packed = lax.all_gather(
        jnp.concatenate([v_block, hidden_cols], axis=2), "fsdp", axis=2, tiled=True
    ).reshape(pair_local, adapter_rank_width, fsdp_size, in_local + 2 * row_local)
    v_full = packed[:, :, :, :in_local].reshape(pair_local, adapter_rank_width, fsdp_size * in_local)
    hidden_all = packed[:, :, :, in_local:].reshape(
        pair_local, adapter_rank_width, fsdp_size, 2, row_local
    )
    hidden_by_shift = jnp.take(hidden_all, (own - shift_ids) % fsdp_size, axis=2).astype(
        jnp.bfloat16
    )
    a_k = jnp.einsum(
        "prskt,spkte->pkre", hidden_by_shift, blocks_by_shift, preferred_element_type=jnp.float32
    )
    base_up = jnp.einsum("pktd,prd->pktr", latents, v_full, precision=highest)
    target_up = jnp.einsum(
        "pktd,prd->pktr", targets, selected_up, preferred_element_type=jnp.float32
    )
    up_gram = jnp.einsum(
        "prd,pqd->prq", selected_up, selected_up, preferred_element_type=jnp.float32
    )
    delta_up = ADAPTER_SCALE * jnp.einsum("pktr,prq->pktq", hidden_f, up_gram, precision=highest)
    partial_err = jnp.sum(
        hidden_f * (base_up - target_up + 0.5 * delta_up), axis=(2, 3)
    ) * (2.0 * ADAPTER_SCALE)
    back = base_up - target_up + delta_up

    onehot = (categories[:, None] == jnp.arange(class_total, dtype=jnp.int32)[None, :]).astype(
        jnp.float32
    )
    errdiff = lax.psum(partial_err, "fsdp") / sample_rows
    kappa = BETA * (0.5 + timesteps.astype(jnp.float32) / 1000.0)
    zvalue = kappa * (errdiff[:, 0] - errdiff[:, 1])
    losses = jax.nn.softplus(zvalue)
    pair_total = jnp.sum(onehot * counts[None, :], axis=1)
    coef_pair = LOSS_SCALE * kappa * jax.nn.sigmoid(zvalue) / pair_total
    signs = jnp.array([2.0, -2.0], dtype=jnp.float32)
    coefficient = coef_pair[:, None] * signs[None, :] / sample_rows

    scale_k = (ADAPTER_SCALE * coefficient)[:, :, None, None]
    hidden_gram = jnp.einsum(
        "pktr,pktq->pkrq", hidden_state, hidden_state, preferred_element_type=jnp.float32
    )
    a_weighted = jnp.sum(scale_k * a_k, axis=1)
    gram_weighted = ADAPTER_SCALE * jnp.sum(scale_k * hidden_gram, axis=1)
    up_t = (
        jnp.einsum("ed,pre->pdr", frozen_weight, a_weighted, precision=highest)
        - jnp.einsum("pktd,pktr->pdr", targets, hidden_f * scale_k, precision=highest)
        + jnp.einsum("pqd,prq->pdr", selected_up, gram_weighted, precision=highest)
    )
    down_t = jnp.einsum("pktd,pktr->pdr", latents, back * scale_k, precision=highest)
    grads = jnp.concatenate([down_t, up_t], axis=2).reshape(
        pair_local, dp_size, col_local, 2 * adapter_rank_width
    )

    gathered = lax.all_to_all(grads.transpose(1, 0, 2, 3), "dp", 0, 0, tiled=True).reshape(
        dp_size * pair_local, col_local * 2 * adapter_rank_width
    )
    dense = jnp.dot(onehot_all.T, gathered, precision=lax.Precision.HIGHEST)
    dense = fsdp_sum(dense, fsdp_size).reshape(class_total, col_local, 2, adapter_rank_width)
    grad_down = dense[:, :, 0].transpose(0, 2, 1)
    grad_up = dense[:, :, 1].transpose(0, 2, 1)
    return (grad_down, grad_up, losses)


def solution(mesh):
    placed = (
        P("dp", None, "fsdp", None),
        P("dp", None, "fsdp", None),
        P("fsdp", None),
        P(None, None, "dp"),
        P(None, None, "dp"),
        P("dp"),
        P("dp"),
    )
    return jax.shard_map(
        local,
        mesh=mesh,
        in_specs=placed,
        out_specs=(P(None, None, "dp"), P(None, None, "dp"), P("dp")),
        check_vma=False,
    )
```

```python
import jax
import jax.numpy as jnp
from jax import lax
from jax.sharding import PartitionSpec as P

ADAPTER_SCALE = 0.5
BETA = 1.0
LOSS_SCALE = 64.0


def fsdp_sum(value, fsdp_size):
    if fsdp_size != 4:
        return lax.psum(value, "fsdp")
    value = value + lax.ppermute(value, "fsdp", [(0, 1), (1, 0), (2, 3), (3, 2)])
    return value + lax.ppermute(value, "fsdp", [(0, 3), (3, 0), (1, 2), (2, 1)])


def local(latents, targets, frozen_weight, adapter_down, adapter_up, categories, timesteps):
    pair_local, _, row_local, feat_width = latents.shape
    class_total, adapter_rank_width, col_local = adapter_down.shape
    fsdp_size = lax.axis_size("fsdp")
    dp_size = lax.axis_size("dp")
    in_local = frozen_weight.shape[0]
    sample_rows = row_local * fsdp_size

    own = lax.axis_index("fsdp")
    shift_ids = jnp.arange(fsdp_size, dtype=jnp.int32)
    latents_split = latents.reshape(pair_local, 2, row_local, fsdp_size, in_local)
    blocks_by_shift = jnp.stack(
        [
            lax.ppermute(
                lax.dynamic_index_in_dim(
                    latents_split, (own + shift) % fsdp_size, axis=3, keepdims=False
                ),
                "fsdp",
                [(src, (src + shift) % fsdp_size) for src in range(fsdp_size)],
            )
            if shift
            else lax.dynamic_index_in_dim(latents_split, own, axis=3, keepdims=False)
            for shift in range(fsdp_size)
        ],
        axis=0,
    )

    cats_all = lax.all_gather(categories, "dp", tiled=True)
    onehot_all = (cats_all[:, None] == jnp.arange(class_total, dtype=jnp.int32)[None, :]).astype(
        jnp.float32
    )
    counts = jnp.sum(onehot_all, axis=0)

    both = jnp.stack([adapter_down, adapter_up], axis=1)
    send = jnp.take(both, cats_all.reshape(dp_size, pair_local), axis=0)
    recv = lax.all_to_all(send, "dp", 0, 0, tiled=True)
    selected = recv.transpose(1, 2, 3, 0, 4).reshape(
        pair_local, 2, adapter_rank_width, dp_size * col_local
    )
    selected_down = selected[:, 0]
    selected_up = selected[:, 1]

    highest = lax.Precision.HIGHEST
    hidden_state = jnp.einsum(
        "pktd,prd->pktr", latents, selected_down, preferred_element_type=jnp.float32
    ).astype(jnp.bfloat16)
    hidden_f = hidden_state.astype(jnp.float32)
    v_block = jnp.einsum(
        "prd,ed->pre", selected_up, frozen_weight, preferred_element_type=jnp.float32
    )
    hidden_cols = hidden_f.transpose(0, 3, 1, 2).reshape(pair_local, adapter_rank_width, 2 * row_local)
    packed = lax.all_gather(
        jnp.concatenate([v_block, hidden_cols], axis=2), "fsdp", axis=2, tiled=True
    ).reshape(pair_local, adapter_rank_width, fsdp_size, in_local + 2 * row_local)
    v_full = packed[:, :, :, :in_local].reshape(pair_local, adapter_rank_width, fsdp_size * in_local)
    hidden_all = packed[:, :, :, in_local:].reshape(
        pair_local, adapter_rank_width, fsdp_size, 2, row_local
    )
    hidden_by_shift = jnp.take(hidden_all, (own - shift_ids) % fsdp_size, axis=2).astype(
        jnp.bfloat16
    )
    a_k = jnp.einsum(
        "prskt,spkte->pkre", hidden_by_shift, blocks_by_shift, preferred_element_type=jnp.float32
    )
    base_up = jnp.einsum("pktd,prd->pktr", latents, v_full, precision=highest)
    target_up = jnp.einsum(
        "pktd,prd->pktr", targets, selected_up, preferred_element_type=jnp.float32
    )
    up_gram = jnp.einsum(
        "prd,pqd->prq", selected_up, selected_up, preferred_element_type=jnp.float32
    )
    delta_up = ADAPTER_SCALE * jnp.einsum("pktr,prq->pktq", hidden_f, up_gram, precision=highest)
    partial_err = jnp.sum(
        hidden_f * (base_up - target_up + 0.5 * delta_up), axis=(2, 3)
    ) * (2.0 * ADAPTER_SCALE)
    back = base_up - target_up + delta_up

    onehot = (categories[:, None] == jnp.arange(class_total, dtype=jnp.int32)[None, :]).astype(
        jnp.float32
    )
    errdiff = lax.psum(partial_err, "fsdp") / sample_rows
    kappa = BETA * (0.5 + timesteps.astype(jnp.float32) / 1000.0)
    zvalue = kappa * (errdiff[:, 0] - errdiff[:, 1])
    losses = jax.nn.softplus(zvalue)
    pair_total = jnp.sum(onehot * counts[None, :], axis=1)
    coef_pair = LOSS_SCALE * kappa * jax.nn.sigmoid(zvalue) / pair_total
    signs = jnp.array([2.0, -2.0], dtype=jnp.float32)
    coefficient = coef_pair[:, None] * signs[None, :] / sample_rows

    scale_k = (ADAPTER_SCALE * coefficient)[:, :, None, None]
    hidden_gram = jnp.einsum(
        "pktr,pktq->pkrq", hidden_state, hidden_state, preferred_element_type=jnp.float32
    )
    a_weighted = jnp.sum(scale_k * a_k, axis=1)
    gram_weighted = ADAPTER_SCALE * jnp.sum(scale_k * hidden_gram, axis=1)
    token_rows = 2 * row_local
    lhs = jnp.concatenate(
        [
            latents.reshape(pair_local, token_rows, feat_width),
            targets.reshape(pair_local, token_rows, feat_width),
            jnp.broadcast_to(frozen_weight[None], (pair_local, in_local, feat_width)),
            selected_up,
        ],
        axis=1,
    )
    zero_tok = jnp.zeros((pair_local, token_rows, adapter_rank_width), jnp.float32)
    zero_in = jnp.zeros((pair_local, in_local, adapter_rank_width), jnp.float32)
    zero_rank = jnp.zeros((pair_local, adapter_rank_width, adapter_rank_width), jnp.float32)
    rhs = jnp.concatenate(
        [
            jnp.concatenate([(back * scale_k).reshape(pair_local, token_rows, -1), zero_tok], axis=2),
            jnp.concatenate([zero_tok, -(hidden_f * scale_k).reshape(pair_local, token_rows, -1)], axis=2),
            jnp.concatenate([zero_in, a_weighted.transpose(0, 2, 1)], axis=2),
            jnp.concatenate([zero_rank, gram_weighted.transpose(0, 2, 1)], axis=2),
        ],
        axis=1,
    )
    grads = jnp.einsum("pjd,pjc->pdc", lhs, rhs, precision=highest).reshape(
        pair_local, dp_size, col_local, 2 * adapter_rank_width
    )

    gathered = lax.all_to_all(grads.transpose(1, 0, 2, 3), "dp", 0, 0, tiled=True).reshape(
        dp_size * pair_local, col_local * 2 * adapter_rank_width
    )
    dense = jnp.dot(onehot_all.T, gathered, precision=lax.Precision.HIGHEST)
    dense = fsdp_sum(dense, fsdp_size).reshape(class_total, col_local, 2, adapter_rank_width)
    grad_down = dense[:, :, 0].transpose(0, 2, 1)
    grad_up = dense[:, :, 1].transpose(0, 2, 1)
    return (grad_down, grad_up, losses)


def solution(mesh):
    placed = (
        P("dp", None, "fsdp", None),
        P("dp", None, "fsdp", None),
        P("fsdp", None),
        P(None, None, "dp"),
        P(None, None, "dp"),
        P("dp"),
        P("dp"),
    )
    return jax.shard_map(
        local,
        mesh=mesh,
        in_specs=placed,
        out_specs=(P(None, None, "dp"), P(None, None, "dp"), P("dp")),
        check_vma=False,
    )
```

```python
import jax
import jax.numpy as jnp
from jax import lax
from jax.sharding import PartitionSpec as P

ADAPTER_SCALE = 0.5
BETA = 1.0
LOSS_SCALE = 64.0


def fsdp_sum(value, fsdp_size):
    if fsdp_size != 4:
        return lax.psum(value, "fsdp")
    value = value + lax.ppermute(value, "fsdp", [(0, 1), (1, 0), (2, 3), (3, 2)])
    return value + lax.ppermute(value, "fsdp", [(0, 3), (3, 0), (1, 2), (2, 1)])


def local(latents, targets, frozen_weight, adapter_down, adapter_up, categories, timesteps):
    pair_local, _, row_local, feat_width = latents.shape
    class_total, adapter_rank_width, col_local = adapter_down.shape
    fsdp_size = lax.axis_size("fsdp")
    dp_size = lax.axis_size("dp")
    in_local = frozen_weight.shape[0]
    sample_rows = row_local * fsdp_size

    own = lax.axis_index("fsdp")
    shift_ids = jnp.arange(fsdp_size, dtype=jnp.int32)
    latents_split = latents.reshape(pair_local, 2, row_local, fsdp_size, in_local)
    blocks_by_shift = jnp.stack(
        [
            lax.ppermute(
                lax.dynamic_index_in_dim(
                    latents_split, (own + shift) % fsdp_size, axis=3, keepdims=False
                ),
                "fsdp",
                [(src, (src + shift) % fsdp_size) for src in range(fsdp_size)],
            )
            if shift
            else lax.dynamic_index_in_dim(latents_split, own, axis=3, keepdims=False)
            for shift in range(fsdp_size)
        ],
        axis=0,
    )

    cats_all = lax.all_gather(categories, "dp", tiled=True)
    onehot_all = (cats_all[:, None] == jnp.arange(class_total, dtype=jnp.int32)[None, :]).astype(
        jnp.float32
    )
    counts = jnp.sum(onehot_all, axis=0)

    both = jnp.stack([adapter_down, adapter_up], axis=1)
    send = jnp.take(both, cats_all.reshape(dp_size, pair_local), axis=0)
    recv = lax.all_to_all(send, "dp", 0, 0, tiled=True)
    selected = recv.transpose(1, 2, 3, 0, 4).reshape(
        pair_local, 2, adapter_rank_width, dp_size * col_local
    )
    selected_down = selected[:, 0]
    selected_up = selected[:, 1]

    highest = lax.Precision.HIGHEST
    hidden_state = jnp.einsum(
        "pktd,prd->pktr", latents, selected_down, preferred_element_type=jnp.float32
    ).astype(jnp.bfloat16)
    hidden_f = hidden_state.astype(jnp.float32)
    v_block = jnp.einsum(
        "prd,ed->pre", selected_up, frozen_weight, preferred_element_type=jnp.float32
    )
    hidden_cols = hidden_f.transpose(0, 3, 1, 2).reshape(pair_local, adapter_rank_width, 2 * row_local)
    packed = lax.all_gather(
        jnp.concatenate([v_block, hidden_cols], axis=2), "fsdp", axis=2, tiled=True
    ).reshape(pair_local, adapter_rank_width, fsdp_size, in_local + 2 * row_local)
    v_full = packed[:, :, :, :in_local].reshape(pair_local, adapter_rank_width, fsdp_size * in_local)
    hidden_all = packed[:, :, :, in_local:].reshape(
        pair_local, adapter_rank_width, fsdp_size, 2, row_local
    )
    hidden_by_shift = jnp.take(hidden_all, (own - shift_ids) % fsdp_size, axis=2).astype(
        jnp.bfloat16
    )
    a_k = jnp.einsum(
        "prskt,spkte->pkre", hidden_by_shift, blocks_by_shift, preferred_element_type=jnp.float32
    )
    base_up = jnp.einsum("pktd,prd->pktr", latents, v_full, precision=highest)
    target_up = jnp.einsum(
        "pktd,prd->pktr", targets, selected_up, preferred_element_type=jnp.float32
    )
    up_gram = jnp.einsum(
        "prd,pqd->prq", selected_up, selected_up, preferred_element_type=jnp.float32
    )
    delta_up = ADAPTER_SCALE * jnp.einsum("pktr,prq->pktq", hidden_f, up_gram, precision=highest)
    partial_err = jnp.sum(
        hidden_f * (base_up - target_up + 0.5 * delta_up), axis=(2, 3)
    ) * (2.0 * ADAPTER_SCALE)
    back = base_up - target_up + delta_up

    onehot = (categories[:, None] == jnp.arange(class_total, dtype=jnp.int32)[None, :]).astype(
        jnp.float32
    )
    errdiff = lax.psum(partial_err, "fsdp") / sample_rows
    kappa = BETA * (0.5 + timesteps.astype(jnp.float32) / 1000.0)
    zvalue = kappa * (errdiff[:, 0] - errdiff[:, 1])
    losses = jax.nn.softplus(zvalue)
    pair_total = jnp.sum(onehot * counts[None, :], axis=1)
    coef_pair = LOSS_SCALE * kappa * jax.nn.sigmoid(zvalue) / pair_total
    signs = jnp.array([2.0, -2.0], dtype=jnp.float32)
    coefficient = coef_pair[:, None] * signs[None, :] / sample_rows

    scale_k = (ADAPTER_SCALE * coefficient)[:, :, None, None]
    hidden_gram = jnp.einsum(
        "pktr,pktq->pkrq", hidden_state, hidden_state, preferred_element_type=jnp.float32
    )
    a_weighted = jnp.sum(scale_k * a_k, axis=1)
    gram_weighted = ADAPTER_SCALE * jnp.sum(scale_k * hidden_gram, axis=1)
    token_rows = 2 * row_local
    lhs = jnp.concatenate(
        [
            latents.reshape(pair_local, token_rows, feat_width),
            targets.reshape(pair_local, token_rows, feat_width),
            jnp.broadcast_to(frozen_weight[None], (pair_local, in_local, feat_width)),
            selected_up,
        ],
        axis=1,
    )
    zero_tok = jnp.zeros((pair_local, token_rows, adapter_rank_width), jnp.float32)
    zero_in = jnp.zeros((pair_local, in_local, adapter_rank_width), jnp.float32)
    zero_rank = jnp.zeros((pair_local, adapter_rank_width, adapter_rank_width), jnp.float32)
    rhs = jnp.concatenate(
        [
            jnp.concatenate([(back * scale_k).reshape(pair_local, token_rows, -1), zero_tok], axis=2),
            jnp.concatenate([zero_tok, -(hidden_f * scale_k).reshape(pair_local, token_rows, -1)], axis=2),
            jnp.concatenate([zero_in, a_weighted.transpose(0, 2, 1)], axis=2),
            jnp.concatenate([zero_rank, gram_weighted.transpose(0, 2, 1)], axis=2),
        ],
        axis=1,
    )
    grads = lax.optimization_barrier(jnp.einsum("pjc,pjd->pcd", rhs, lhs, precision=highest))
    grads = grads.reshape(pair_local, 2 * adapter_rank_width, dp_size, col_local).transpose(0, 2, 3, 1)

    gathered = lax.all_to_all(grads.transpose(1, 0, 2, 3), "dp", 0, 0, tiled=True).reshape(
        dp_size * pair_local, col_local * 2 * adapter_rank_width
    )
    dense = jnp.dot(onehot_all.T, gathered, precision=lax.Precision.HIGHEST)
    dense = fsdp_sum(dense, fsdp_size).reshape(class_total, col_local, 2, adapter_rank_width)
    grad_down = dense[:, :, 0].transpose(0, 2, 1)
    grad_up = dense[:, :, 1].transpose(0, 2, 1)
    return (grad_down, grad_up, losses)


def solution(mesh):
    placed = (
        P("dp", None, "fsdp", None),
        P("dp", None, "fsdp", None),
        P("fsdp", None),
        P(None, None, "dp"),
        P(None, None, "dp"),
        P("dp"),
        P("dp"),
    )
    return jax.shard_map(
        local,
        mesh=mesh,
        in_specs=placed,
        out_specs=(P(None, None, "dp"), P(None, None, "dp"), P("dp")),
        check_vma=False,
    )
```

```python
import jax
import jax.numpy as jnp
from jax import lax
from jax.sharding import PartitionSpec as P

ADAPTER_SCALE = 0.5
BETA = 1.0
LOSS_SCALE = 64.0


def fsdp_sum(value, fsdp_size):
    shifted = [value] + [
        lax.ppermute(value, "fsdp", [(src, (src + shift) % fsdp_size) for src in range(fsdp_size)])
        for shift in range(1, fsdp_size)
    ]
    own = lax.axis_index("fsdp")
    doubled = jnp.stack(shifted[::-1] + shifted[::-1], axis=0)
    by_source = lax.dynamic_slice_in_dim(doubled, (fsdp_size - 1 - own) % fsdp_size, fsdp_size, 0)
    total = by_source[0]
    for index in range(1, fsdp_size):
        total = total + by_source[index]
    return total


def local(latents, targets, frozen_weight, adapter_down, adapter_up, categories, timesteps):
    pair_local, _, row_local, feat_width = latents.shape
    class_total, adapter_rank_width, col_local = adapter_down.shape
    fsdp_size = lax.axis_size("fsdp")
    dp_size = lax.axis_size("dp")
    in_local = frozen_weight.shape[0]
    sample_rows = row_local * fsdp_size

    own = lax.axis_index("fsdp")
    shift_ids = jnp.arange(fsdp_size, dtype=jnp.int32)
    latents_split = latents.reshape(pair_local, 2, row_local, fsdp_size, in_local)
    blocks_by_shift = jnp.stack(
        [
            lax.ppermute(
                lax.dynamic_index_in_dim(
                    latents_split, (own + shift) % fsdp_size, axis=3, keepdims=False
                ),
                "fsdp",
                [(src, (src + shift) % fsdp_size) for src in range(fsdp_size)],
            )
            if shift
            else lax.dynamic_index_in_dim(latents_split, own, axis=3, keepdims=False)
            for shift in range(fsdp_size)
        ],
        axis=0,
    )

    cats_all = lax.all_gather(categories, "dp", tiled=True)
    onehot_all = (cats_all[:, None] == jnp.arange(class_total, dtype=jnp.int32)[None, :]).astype(
        jnp.float32
    )
    counts = jnp.sum(onehot_all, axis=0)

    both = jnp.stack([adapter_down, adapter_up], axis=1)
    send = jnp.take(both, cats_all.reshape(dp_size, pair_local), axis=0)
    recv = lax.all_to_all(send, "dp", 0, 0, tiled=True)
    selected = recv.transpose(1, 2, 3, 0, 4).reshape(
        pair_local, 2, adapter_rank_width, dp_size * col_local
    )
    selected_down = selected[:, 0]
    selected_up = selected[:, 1]

    highest = lax.Precision.HIGHEST
    hidden_state = jnp.einsum(
        "pktd,prd->pktr", latents, selected_down, preferred_element_type=jnp.float32
    ).astype(jnp.bfloat16)
    hidden_f = hidden_state.astype(jnp.float32)
    v_block = jnp.einsum(
        "prd,ed->pre", selected_up, frozen_weight, preferred_element_type=jnp.float32
    )
    hidden_cols = hidden_f.transpose(0, 3, 1, 2).reshape(pair_local, adapter_rank_width, 2 * row_local)
    packed = lax.all_gather(
        jnp.concatenate([v_block, hidden_cols], axis=2), "fsdp", axis=2, tiled=True
    ).reshape(pair_local, adapter_rank_width, fsdp_size, in_local + 2 * row_local)
    v_full = packed[:, :, :, :in_local].reshape(pair_local, adapter_rank_width, fsdp_size * in_local)
    hidden_all = packed[:, :, :, in_local:].reshape(
        pair_local, adapter_rank_width, fsdp_size, 2, row_local
    )
    hidden_by_shift = jnp.take(hidden_all, (own - shift_ids) % fsdp_size, axis=2).astype(
        jnp.bfloat16
    )
    a_k = jnp.einsum(
        "prskt,spkte->pkre", hidden_by_shift, blocks_by_shift, preferred_element_type=jnp.float32
    )
    base_up = jnp.einsum("pktd,prd->pktr", latents, v_full, precision=highest)
    target_up = jnp.einsum(
        "pktd,prd->pktr", targets, selected_up, preferred_element_type=jnp.float32
    )
    up_gram = jnp.einsum(
        "prd,pqd->prq", selected_up, selected_up, preferred_element_type=jnp.float32
    )
    delta_up = ADAPTER_SCALE * jnp.einsum("pktr,prq->pktq", hidden_f, up_gram, precision=highest)
    partial_err = jnp.sum(
        hidden_f * (base_up - target_up + 0.5 * delta_up), axis=(2, 3)
    ) * (2.0 * ADAPTER_SCALE)
    back = base_up - target_up + delta_up

    onehot = (categories[:, None] == jnp.arange(class_total, dtype=jnp.int32)[None, :]).astype(
        jnp.float32
    )
    errdiff = lax.psum(partial_err, "fsdp") / sample_rows
    kappa = BETA * (0.5 + timesteps.astype(jnp.float32) / 1000.0)
    zvalue = kappa * (errdiff[:, 0] - errdiff[:, 1])
    losses = jax.nn.softplus(zvalue)
    pair_total = jnp.sum(onehot * counts[None, :], axis=1)
    coef_pair = LOSS_SCALE * kappa * jax.nn.sigmoid(zvalue) / pair_total
    signs = jnp.array([2.0, -2.0], dtype=jnp.float32)
    coefficient = coef_pair[:, None] * signs[None, :] / sample_rows

    scale_k = (ADAPTER_SCALE * coefficient)[:, :, None, None]
    hidden_gram = jnp.einsum(
        "pktr,pktq->pkrq", hidden_state, hidden_state, preferred_element_type=jnp.float32
    )
    a_weighted = jnp.sum(scale_k * a_k, axis=1)
    gram_weighted = ADAPTER_SCALE * jnp.sum(scale_k * hidden_gram, axis=1)
    token_rows = 2 * row_local
    lhs = jnp.concatenate(
        [
            latents.reshape(pair_local, token_rows, feat_width),
            targets.reshape(pair_local, token_rows, feat_width),
            jnp.broadcast_to(frozen_weight[None], (pair_local, in_local, feat_width)),
            selected_up,
        ],
        axis=1,
    )
    zero_tok = jnp.zeros((pair_local, token_rows, adapter_rank_width), jnp.float32)
    zero_in = jnp.zeros((pair_local, in_local, adapter_rank_width), jnp.float32)
    zero_rank = jnp.zeros((pair_local, adapter_rank_width, adapter_rank_width), jnp.float32)
    rhs = jnp.concatenate(
        [
            jnp.concatenate([(back * scale_k).reshape(pair_local, token_rows, -1), zero_tok], axis=2),
            jnp.concatenate([zero_tok, -(hidden_f * scale_k).reshape(pair_local, token_rows, -1)], axis=2),
            jnp.concatenate([zero_in, a_weighted.transpose(0, 2, 1)], axis=2),
            jnp.concatenate([zero_rank, gram_weighted.transpose(0, 2, 1)], axis=2),
        ],
        axis=1,
    )
    grads = lax.optimization_barrier(jnp.einsum("pjc,pjd->pcd", rhs, lhs, precision=highest))
    grads = grads.reshape(pair_local, 2 * adapter_rank_width, dp_size, col_local).transpose(0, 2, 3, 1)

    gathered = lax.all_to_all(grads.transpose(1, 0, 2, 3), "dp", 0, 0, tiled=True).reshape(
        dp_size * pair_local, col_local * 2 * adapter_rank_width
    )
    dense = jnp.dot(onehot_all.T, gathered, precision=lax.Precision.HIGHEST)
    dense = fsdp_sum(dense, fsdp_size).reshape(class_total, col_local, 2, adapter_rank_width)
    grad_down = dense[:, :, 0].transpose(0, 2, 1)
    grad_up = dense[:, :, 1].transpose(0, 2, 1)
    return (grad_down, grad_up, losses)


def solution(mesh):
    placed = (
        P("dp", None, "fsdp", None),
        P("dp", None, "fsdp", None),
        P("fsdp", None),
        P(None, None, "dp"),
        P(None, None, "dp"),
        P("dp"),
        P("dp"),
    )
    return jax.shard_map(
        local,
        mesh=mesh,
        in_specs=placed,
        out_specs=(P(None, None, "dp"), P(None, None, "dp"), P("dp")),
        check_vma=False,
    )
```

```python
import jax
import jax.numpy as jnp
from jax import lax
from jax.sharding import PartitionSpec as P

ADAPTER_SCALE = 0.5
BETA = 1.0
LOSS_SCALE = 64.0


def fsdp_sum(value, fsdp_size):
    shifted = [value] + [
        lax.ppermute(value, "fsdp", [(src, (src + shift) % fsdp_size) for src in range(fsdp_size)])
        for shift in range(1, fsdp_size)
    ]
    own = lax.axis_index("fsdp")
    doubled = jnp.stack(shifted[::-1] + shifted[::-1], axis=0)
    by_source = lax.dynamic_slice_in_dim(doubled, (fsdp_size - 1 - own) % fsdp_size, fsdp_size, 0)
    total = by_source[0]
    for index in range(1, fsdp_size):
        total = total + by_source[index]
    return total


def local(latents, targets, frozen_weight, adapter_down, adapter_up, categories, timesteps):
    pair_local, _, row_local, feat_width = latents.shape
    class_total, adapter_rank_width, col_local = adapter_down.shape
    fsdp_size = lax.axis_size("fsdp")
    dp_size = lax.axis_size("dp")
    in_local = frozen_weight.shape[0]
    sample_rows = row_local * fsdp_size

    own = lax.axis_index("fsdp")
    shift_ids = jnp.arange(fsdp_size, dtype=jnp.int32)
    latents_split = latents.reshape(pair_local, 2, row_local, fsdp_size, in_local)
    blocks_by_shift = jnp.stack(
        [
            lax.ppermute(
                lax.dynamic_index_in_dim(
                    latents_split, (own + shift) % fsdp_size, axis=3, keepdims=False
                ),
                "fsdp",
                [(src, (src + shift) % fsdp_size) for src in range(fsdp_size)],
            )
            if shift
            else lax.dynamic_index_in_dim(latents_split, own, axis=3, keepdims=False)
            for shift in range(fsdp_size)
        ],
        axis=0,
    )

    cats_all = lax.all_gather(categories, "dp", tiled=True)
    onehot_all = (cats_all[:, None] == jnp.arange(class_total, dtype=jnp.int32)[None, :]).astype(
        jnp.float32
    )
    counts = jnp.sum(onehot_all, axis=0)

    both = jnp.stack([adapter_down, adapter_up], axis=1)
    send = jnp.take(both, cats_all.reshape(dp_size, pair_local), axis=0)
    recv = lax.all_to_all(send, "dp", 0, 0, tiled=True)
    selected = recv.transpose(1, 2, 3, 0, 4).reshape(
        pair_local, 2, adapter_rank_width, dp_size * col_local
    )
    selected_down = selected[:, 0]
    selected_up = selected[:, 1]

    highest = lax.Precision.HIGHEST
    hidden_state = jnp.einsum(
        "pktd,prd->pktr", latents, selected_down, preferred_element_type=jnp.float32
    ).astype(jnp.bfloat16)
    hidden_f = hidden_state.astype(jnp.float32)
    v_block = jnp.einsum(
        "prd,ed->pre", selected_up, frozen_weight, preferred_element_type=jnp.float32
    )
    hidden_cols = hidden_f.transpose(0, 3, 1, 2).reshape(pair_local, adapter_rank_width, 2 * row_local)
    packed = lax.all_gather(
        jnp.concatenate([v_block, hidden_cols], axis=2), "fsdp", axis=2, tiled=True
    ).reshape(pair_local, adapter_rank_width, fsdp_size, in_local + 2 * row_local)
    v_full = packed[:, :, :, :in_local].reshape(pair_local, adapter_rank_width, fsdp_size * in_local)
    hidden_all = packed[:, :, :, in_local:].reshape(
        pair_local, adapter_rank_width, fsdp_size, 2, row_local
    )
    hidden_by_shift = jnp.take(hidden_all, (own - shift_ids) % fsdp_size, axis=2).astype(
        jnp.bfloat16
    )
    a_k = jnp.einsum(
        "prskt,spkte->pkre", hidden_by_shift, blocks_by_shift, preferred_element_type=jnp.float32
    )
    base_up = jnp.einsum("pktd,prd->pktr", latents, v_full, precision=highest)
    target_up = jnp.einsum(
        "pktd,prd->pktr", targets, selected_up, preferred_element_type=jnp.float32
    )
    up_gram = jnp.einsum(
        "prd,pqd->prq", selected_up, selected_up, preferred_element_type=jnp.float32
    )
    delta_up = ADAPTER_SCALE * jnp.einsum("pktr,prq->pktq", hidden_f, up_gram, precision=highest)
    partial_err = jnp.sum(
        hidden_f * (base_up - target_up + 0.5 * delta_up), axis=(2, 3)
    ) * (2.0 * ADAPTER_SCALE)
    back = base_up - target_up + delta_up

    onehot = (categories[:, None] == jnp.arange(class_total, dtype=jnp.int32)[None, :]).astype(
        jnp.float32
    )
    errdiff = fsdp_sum(partial_err, fsdp_size) / sample_rows
    kappa = BETA * (0.5 + timesteps.astype(jnp.float32) / 1000.0)
    zvalue = kappa * (errdiff[:, 0] - errdiff[:, 1])
    losses = jax.nn.softplus(zvalue)
    pair_total = jnp.sum(onehot * counts[None, :], axis=1)
    coef_pair = LOSS_SCALE * kappa * jax.nn.sigmoid(zvalue) / pair_total
    signs = jnp.array([2.0, -2.0], dtype=jnp.float32)
    coefficient = coef_pair[:, None] * signs[None, :] / sample_rows

    scale_k = (ADAPTER_SCALE * coefficient)[:, :, None, None]
    hidden_gram = jnp.einsum(
        "pktr,pktq->pkrq", hidden_state, hidden_state, preferred_element_type=jnp.float32
    )
    a_weighted = jnp.sum(scale_k * a_k, axis=1)
    gram_weighted = ADAPTER_SCALE * jnp.sum(scale_k * hidden_gram, axis=1)
    token_rows = 2 * row_local
    lhs = jnp.concatenate(
        [
            latents.reshape(pair_local, token_rows, feat_width),
            targets.reshape(pair_local, token_rows, feat_width),
            jnp.broadcast_to(frozen_weight[None], (pair_local, in_local, feat_width)),
            selected_up,
        ],
        axis=1,
    )
    zero_tok = jnp.zeros((pair_local, token_rows, adapter_rank_width), jnp.float32)
    zero_in = jnp.zeros((pair_local, in_local, adapter_rank_width), jnp.float32)
    zero_rank = jnp.zeros((pair_local, adapter_rank_width, adapter_rank_width), jnp.float32)
    rhs = jnp.concatenate(
        [
            jnp.concatenate([(back * scale_k).reshape(pair_local, token_rows, -1), zero_tok], axis=2),
            jnp.concatenate([zero_tok, -(hidden_f * scale_k).reshape(pair_local, token_rows, -1)], axis=2),
            jnp.concatenate([zero_in, a_weighted.transpose(0, 2, 1)], axis=2),
            jnp.concatenate([zero_rank, gram_weighted.transpose(0, 2, 1)], axis=2),
        ],
        axis=1,
    )
    grads = lax.optimization_barrier(jnp.einsum("pjc,pjd->pcd", rhs, lhs, precision=highest))
    grads = grads.reshape(pair_local, 2 * adapter_rank_width, dp_size, col_local).transpose(0, 2, 3, 1)

    gathered = lax.all_to_all(grads.transpose(1, 0, 2, 3), "dp", 0, 0, tiled=True).reshape(
        dp_size * pair_local, col_local * 2 * adapter_rank_width
    )
    dense = jnp.dot(onehot_all.T, gathered, precision=lax.Precision.HIGHEST)
    dense = fsdp_sum(dense, fsdp_size).reshape(class_total, col_local, 2, adapter_rank_width)
    grad_down = dense[:, :, 0].transpose(0, 2, 1)
    grad_up = dense[:, :, 1].transpose(0, 2, 1)
    return (grad_down, grad_up, losses)


def solution(mesh):
    placed = (
        P("dp", None, "fsdp", None),
        P("dp", None, "fsdp", None),
        P("fsdp", None),
        P(None, None, "dp"),
        P(None, None, "dp"),
        P("dp"),
        P("dp"),
    )
    return jax.shard_map(
        local,
        mesh=mesh,
        in_specs=placed,
        out_specs=(P(None, None, "dp"), P(None, None, "dp"), P("dp")),
        check_vma=False,
    )
```

```python
import jax
import jax.numpy as jnp
from jax import lax
from jax.sharding import PartitionSpec as P

ADAPTER_SCALE = 0.5
BETA = 1.0
LOSS_SCALE = 64.0


def fsdp_sum(value, fsdp_size):
    shifted = [value] + [
        lax.ppermute(value, "fsdp", [(src, (src + shift) % fsdp_size) for src in range(fsdp_size)])
        for shift in range(1, fsdp_size)
    ]
    own = lax.axis_index("fsdp")
    doubled = jnp.stack(shifted[::-1] + shifted[::-1], axis=0)
    by_source = lax.dynamic_slice_in_dim(doubled, (fsdp_size - 1 - own) % fsdp_size, fsdp_size, 0)
    total = by_source[0]
    for index in range(1, fsdp_size):
        total = total + by_source[index]
    return total


def local(latents, targets, frozen_weight, adapter_down, adapter_up, categories, timesteps):
    pair_local, _, row_local, feat_width = latents.shape
    class_total, adapter_rank_width, col_local = adapter_down.shape
    fsdp_size = lax.axis_size("fsdp")
    dp_size = lax.axis_size("dp")
    in_local = frozen_weight.shape[0]
    sample_rows = row_local * fsdp_size

    own = lax.axis_index("fsdp")
    shift_ids = jnp.arange(fsdp_size, dtype=jnp.int32)
    latents_split = latents.reshape(pair_local, 2, row_local, fsdp_size, in_local)
    blocks_by_shift = jnp.stack(
        [
            lax.ppermute(
                lax.dynamic_index_in_dim(
                    latents_split, (own + shift) % fsdp_size, axis=3, keepdims=False
                ),
                "fsdp",
                [(src, (src + shift) % fsdp_size) for src in range(fsdp_size)],
            )
            if shift
            else lax.dynamic_index_in_dim(latents_split, own, axis=3, keepdims=False)
            for shift in range(fsdp_size)
        ],
        axis=0,
    )

    cats_all = lax.all_gather(categories, "dp", tiled=True)
    onehot_all = (cats_all[:, None] == jnp.arange(class_total, dtype=jnp.int32)[None, :]).astype(
        jnp.float32
    )
    counts = jnp.sum(onehot_all, axis=0)

    both = jnp.stack([adapter_down, adapter_up], axis=1)
    send = jnp.take(both, cats_all.reshape(dp_size, pair_local), axis=0)
    recv = lax.all_to_all(send, "dp", 0, 0, tiled=True)
    selected = recv.transpose(1, 2, 3, 0, 4).reshape(
        pair_local, 2, adapter_rank_width, dp_size * col_local
    )
    selected_down = selected[:, 0]
    selected_up = selected[:, 1]

    highest = lax.Precision.HIGHEST
    hidden_state = jnp.einsum(
        "pktd,prd->pktr", latents, selected_down, preferred_element_type=jnp.float32
    ).astype(jnp.bfloat16)
    hidden_f = hidden_state.astype(jnp.float32)
    v_block = jnp.einsum(
        "prd,ed->pre", selected_up, frozen_weight, preferred_element_type=jnp.float32
    )
    hidden_cols = hidden_f.transpose(0, 3, 1, 2).reshape(pair_local, adapter_rank_width, 2 * row_local)
    packed = lax.all_gather(
        jnp.concatenate([v_block, hidden_cols], axis=2), "fsdp", axis=2, tiled=True
    ).reshape(pair_local, adapter_rank_width, fsdp_size, in_local + 2 * row_local)
    v_full = packed[:, :, :, :in_local].reshape(pair_local, adapter_rank_width, fsdp_size * in_local)
    hidden_all = packed[:, :, :, in_local:].reshape(
        pair_local, adapter_rank_width, fsdp_size, 2, row_local
    )
    hidden_by_shift = jnp.take(hidden_all, (own - shift_ids) % fsdp_size, axis=2).astype(
        jnp.bfloat16
    )
    a_k = jnp.einsum(
        "prskt,spkte->pkre", hidden_by_shift, blocks_by_shift, preferred_element_type=jnp.float32
    )
    base_up = jnp.einsum("pktd,prd->pktr", latents, v_full, precision=highest)
    target_up = jnp.einsum(
        "pktd,prd->pktr", targets, selected_up, preferred_element_type=jnp.float32
    )
    up_gram = jnp.einsum(
        "prd,pqd->prq", selected_up, selected_up, preferred_element_type=jnp.float32
    )
    delta_up = ADAPTER_SCALE * jnp.einsum("pktr,prq->pktq", hidden_f, up_gram, precision=highest)
    partial_err = jnp.sum(
        hidden_f * (base_up - target_up + 0.5 * delta_up), axis=(2, 3)
    ) * (2.0 * ADAPTER_SCALE)
    back = base_up - target_up + delta_up

    onehot = (categories[:, None] == jnp.arange(class_total, dtype=jnp.int32)[None, :]).astype(
        jnp.float32
    )
    errdiff = lax.psum(partial_err, "fsdp") / sample_rows
    kappa = BETA * (0.5 + timesteps.astype(jnp.float32) / 1000.0)
    zvalue = kappa * (errdiff[:, 0] - errdiff[:, 1])
    losses = jax.nn.softplus(zvalue)
    pair_total = jnp.sum(onehot * counts[None, :], axis=1)
    coef_pair = LOSS_SCALE * kappa * jax.nn.sigmoid(zvalue) / pair_total
    signs = jnp.array([2.0, -2.0], dtype=jnp.float32)
    coefficient = coef_pair[:, None] * signs[None, :] / sample_rows

    scale_k = (ADAPTER_SCALE * coefficient)[:, :, None, None]
    hidden_gram = jnp.einsum(
        "pktr,pktq->pkrq", hidden_state, hidden_state, preferred_element_type=jnp.float32
    )
    a_weighted = jnp.sum(scale_k * a_k, axis=1)
    gram_weighted = ADAPTER_SCALE * jnp.sum(scale_k * hidden_gram, axis=1)
    token_rows = 2 * row_local
    lhs = jnp.concatenate(
        [
            latents.reshape(pair_local, token_rows, feat_width),
            targets.reshape(pair_local, token_rows, feat_width),
            jnp.broadcast_to(frozen_weight[None], (pair_local, in_local, feat_width)),
            selected_up,
        ],
        axis=1,
    )
    zero_tok = jnp.zeros((pair_local, token_rows, adapter_rank_width), jnp.float32)
    zero_in = jnp.zeros((pair_local, in_local, adapter_rank_width), jnp.float32)
    zero_rank = jnp.zeros((pair_local, adapter_rank_width, adapter_rank_width), jnp.float32)
    rhs = jnp.concatenate(
        [
            jnp.concatenate([(back * scale_k).reshape(pair_local, token_rows, -1), zero_tok], axis=2),
            jnp.concatenate([zero_tok, -(hidden_f * scale_k).reshape(pair_local, token_rows, -1)], axis=2),
            jnp.concatenate([zero_in, a_weighted.transpose(0, 2, 1)], axis=2),
            jnp.concatenate([zero_rank, gram_weighted.transpose(0, 2, 1)], axis=2),
        ],
        axis=1,
    )
    rhs_high = rhs.astype(jnp.bfloat16)
    rhs_low = (rhs - rhs_high.astype(jnp.float32)).astype(jnp.bfloat16)
    grads = lax.optimization_barrier(
        jnp.einsum("pjc,pjd->pcd", rhs_high, lhs, preferred_element_type=jnp.float32)
        + jnp.einsum("pjc,pjd->pcd", rhs_low, lhs, preferred_element_type=jnp.float32)
    )
    grads = grads.reshape(pair_local, 2 * adapter_rank_width, dp_size, col_local).transpose(0, 2, 3, 1)

    gathered = lax.all_to_all(grads.transpose(1, 0, 2, 3), "dp", 0, 0, tiled=True).reshape(
        dp_size * pair_local, col_local * 2 * adapter_rank_width
    )
    dense = jnp.dot(onehot_all.T, gathered, precision=lax.Precision.HIGHEST)
    dense = fsdp_sum(dense, fsdp_size).reshape(class_total, col_local, 2, adapter_rank_width)
    grad_down = dense[:, :, 0].transpose(0, 2, 1)
    grad_up = dense[:, :, 1].transpose(0, 2, 1)
    return (grad_down, grad_up, losses)


def solution(mesh):
    placed = (
        P("dp", None, "fsdp", None),
        P("dp", None, "fsdp", None),
        P("fsdp", None),
        P(None, None, "dp"),
        P(None, None, "dp"),
        P("dp"),
        P("dp"),
    )
    return jax.shard_map(
        local,
        mesh=mesh,
        in_specs=placed,
        out_specs=(P(None, None, "dp"), P(None, None, "dp"), P("dp")),
        check_vma=False,
    )
```

```python
import jax
import jax.numpy as jnp
from jax import lax
from jax.sharding import PartitionSpec as P

ADAPTER_SCALE = 0.5
BETA = 1.0
LOSS_SCALE = 64.0


def fsdp_sum(value, fsdp_size):
    shifted = [value] + [
        lax.ppermute(value, "fsdp", [(src, (src + shift) % fsdp_size) for src in range(fsdp_size)])
        for shift in range(1, fsdp_size)
    ]
    own = lax.axis_index("fsdp")
    doubled = jnp.stack(shifted[::-1] + shifted[::-1], axis=0)
    by_source = lax.dynamic_slice_in_dim(doubled, (fsdp_size - 1 - own) % fsdp_size, fsdp_size, 0)
    total = by_source[0]
    for index in range(1, fsdp_size):
        total = total + by_source[index]
    return total


def local(latents, targets, frozen_weight, adapter_down, adapter_up, categories, timesteps):
    pair_local, _, row_local, feat_width = latents.shape
    class_total, adapter_rank_width, col_local = adapter_down.shape
    fsdp_size = lax.axis_size("fsdp")
    dp_size = lax.axis_size("dp")
    in_local = frozen_weight.shape[0]
    sample_rows = row_local * fsdp_size

    own = lax.axis_index("fsdp")
    shift_ids = jnp.arange(fsdp_size, dtype=jnp.int32)
    latents_split = latents.reshape(pair_local, 2, row_local, fsdp_size, in_local)
    blocks_by_shift = jnp.stack(
        [
            lax.ppermute(
                lax.dynamic_index_in_dim(
                    latents_split, (own + shift) % fsdp_size, axis=3, keepdims=False
                ),
                "fsdp",
                [(src, (src + shift) % fsdp_size) for src in range(fsdp_size)],
            )
            if shift
            else lax.dynamic_index_in_dim(latents_split, own, axis=3, keepdims=False)
            for shift in range(fsdp_size)
        ],
        axis=0,
    )

    cats_all = lax.all_gather(categories, "dp", tiled=True)
    onehot_all = (cats_all[:, None] == jnp.arange(class_total, dtype=jnp.int32)[None, :]).astype(
        jnp.float32
    )
    counts = jnp.sum(onehot_all, axis=0)

    both = jnp.stack([adapter_down, adapter_up], axis=1)
    send = jnp.take(both, cats_all.reshape(dp_size, pair_local), axis=0)
    recv = lax.all_to_all(send, "dp", 0, 0, tiled=True)
    selected = recv.transpose(1, 2, 3, 0, 4).reshape(
        pair_local, 2, adapter_rank_width, dp_size * col_local
    )
    selected_down = selected[:, 0]
    selected_up = selected[:, 1]

    highest = lax.Precision.HIGHEST
    hidden_state = jnp.einsum(
        "pktd,prd->pktr", latents, selected_down, preferred_element_type=jnp.float32
    ).astype(jnp.bfloat16)
    hidden_f = hidden_state.astype(jnp.float32)
    v_block = jnp.einsum(
        "prd,ed->pre", selected_up, frozen_weight, preferred_element_type=jnp.float32
    )
    hidden_cols = hidden_f.transpose(0, 3, 1, 2).reshape(pair_local, adapter_rank_width, 2 * row_local)
    packed = lax.all_gather(
        jnp.concatenate([v_block, hidden_cols], axis=2), "fsdp", axis=2, tiled=True
    ).reshape(pair_local, adapter_rank_width, fsdp_size, in_local + 2 * row_local)
    v_full = packed[:, :, :, :in_local].reshape(pair_local, adapter_rank_width, fsdp_size * in_local)
    hidden_all = packed[:, :, :, in_local:].reshape(
        pair_local, adapter_rank_width, fsdp_size, 2, row_local
    )
    hidden_by_shift = jnp.take(hidden_all, (own - shift_ids) % fsdp_size, axis=2).astype(
        jnp.bfloat16
    )
    a_k = jnp.einsum(
        "prskt,spkte->pkre", hidden_by_shift, blocks_by_shift, preferred_element_type=jnp.float32
    )
    base_up = jnp.einsum("pktd,prd->pktr", latents, v_full, precision=highest)
    target_up = jnp.einsum(
        "pktd,prd->pktr", targets, selected_up, preferred_element_type=jnp.float32
    )
    up_gram = jnp.einsum(
        "prd,pqd->prq", selected_up, selected_up, preferred_element_type=jnp.float32
    )
    delta_up = ADAPTER_SCALE * jnp.einsum("pktr,prq->pktq", hidden_f, up_gram, precision=highest)
    partial_err = jnp.sum(
        hidden_f * (base_up - target_up + 0.5 * delta_up), axis=(2, 3)
    ) * (2.0 * ADAPTER_SCALE)
    back = base_up - target_up + delta_up

    onehot = (categories[:, None] == jnp.arange(class_total, dtype=jnp.int32)[None, :]).astype(
        jnp.float32
    )
    errdiff = lax.psum(partial_err, "fsdp") / sample_rows
    kappa = BETA * (0.5 + timesteps.astype(jnp.float32) / 1000.0)
    zvalue = kappa * (errdiff[:, 0] - errdiff[:, 1])
    losses = jax.nn.softplus(zvalue)
    pair_total = jnp.sum(onehot * counts[None, :], axis=1)
    coef_pair = LOSS_SCALE * kappa * jax.nn.sigmoid(zvalue) / pair_total
    signs = jnp.array([2.0, -2.0], dtype=jnp.float32)
    coefficient = coef_pair[:, None] * signs[None, :] / sample_rows

    scale_k = (ADAPTER_SCALE * coefficient)[:, :, None, None]
    hidden_gram = jnp.einsum(
        "pktr,pktq->pkrq", hidden_state, hidden_state, preferred_element_type=jnp.float32
    )
    a_weighted = jnp.sum(scale_k * a_k, axis=1)
    gram_weighted = ADAPTER_SCALE * jnp.sum(scale_k * hidden_gram, axis=1)
    token_rows = 2 * row_local
    lhs = jnp.concatenate(
        [
            latents.reshape(pair_local, token_rows, feat_width),
            targets.reshape(pair_local, token_rows, feat_width),
            selected_up,
        ],
        axis=1,
    )
    zero_tok = jnp.zeros((pair_local, token_rows, adapter_rank_width), jnp.float32)
    zero_rank = jnp.zeros((pair_local, adapter_rank_width, adapter_rank_width), jnp.float32)
    rhs = jnp.concatenate(
        [
            jnp.concatenate([(back * scale_k).reshape(pair_local, token_rows, -1), zero_tok], axis=2),
            jnp.concatenate([zero_tok, -(hidden_f * scale_k).reshape(pair_local, token_rows, -1)], axis=2),
            jnp.concatenate([zero_rank, gram_weighted.transpose(0, 2, 1)], axis=2),
        ],
        axis=1,
    )
    small = jnp.einsum("pjc,pjd->pcd", rhs, lhs, precision=highest)
    w_term = jnp.einsum("pre,ed->prd", a_weighted, frozen_weight, precision=highest)
    grads = lax.optimization_barrier(
        jnp.concatenate(
            [small[:, :adapter_rank_width], small[:, adapter_rank_width:] + w_term], axis=1
        )
    )
    grads = grads.reshape(pair_local, 2 * adapter_rank_width, dp_size, col_local).transpose(0, 2, 3, 1)

    gathered = lax.all_to_all(grads.transpose(1, 0, 2, 3), "dp", 0, 0, tiled=True).reshape(
        dp_size * pair_local, col_local * 2 * adapter_rank_width
    )
    dense = jnp.dot(onehot_all.T, gathered, precision=lax.Precision.HIGHEST)
    dense = fsdp_sum(dense, fsdp_size).reshape(class_total, col_local, 2, adapter_rank_width)
    grad_down = dense[:, :, 0].transpose(0, 2, 1)
    grad_up = dense[:, :, 1].transpose(0, 2, 1)
    return (grad_down, grad_up, losses)


def solution(mesh):
    placed = (
        P("dp", None, "fsdp", None),
        P("dp", None, "fsdp", None),
        P("fsdp", None),
        P(None, None, "dp"),
        P(None, None, "dp"),
        P("dp"),
        P("dp"),
    )
    return jax.shard_map(
        local,
        mesh=mesh,
        in_specs=placed,
        out_specs=(P(None, None, "dp"), P(None, None, "dp"), P("dp")),
        check_vma=False,
    )
```
